128 devices in a mesh: seq: 32 (over x, z, core), tp: 4 (over y).
Axes of the slice: x: 4, y: 4, z: 4, core: 2. Of those that a mesh axis runs over, the one named last changes fastest.
Arguments:
- tokens: bfloat16 [8192, 2048], P('seq'), may hold values from -6 to 6
- attn_gain: float32 [2048], replicated, may hold values from 0.25 to 1.75
- q_weight: bfloat16 [2048, 3072], P(None, 'tp'), may hold values from -16.744559 to 16.744559
- kva_weight: bfloat16 [2048, 576], replicated, may hold values from -0.176776695 to 0.176776695
- kv_gain: float32 [512], replicated, may hold values from 0.25 to 1.75
- kvb_weight: bfloat16 [512, 4096], P(None, 'tp'), may hold values from -0.25 to 0.25
- o_weight: bfloat16 [2048, 2048], P('tp'), may hold values from -0.125 to 0.125
- ffn_gain: float32 [2048], replicated, may hold values from 0.25 to 1.75
- shared_gate_up: bfloat16 [2, 2048, 2816], P(None, None, 'tp'), may hold values from -0.125 to 0.125
- shared_down: bfloat16 [2816, 2048], P('tp'), may hold values from -0.109375 to 0.109375
- expert_gate_up: bfloat16 [32, 2, 2048, 1408], P('seq', None, None, 'tp'), may hold values from -0.125 to 0.125
- expert_down: bfloat16 [32, 1408, 2048], P('seq', 'tp'), may hold values from -0.15625 to 0.15625
- expert_ids: int32 [8192, 6], P('seq'), may hold values from 0 to 31, all different within a row; in each aligned block of 256 rows (0 to 255, 256 to 511, ...) at most 64 rows name the same one
- route_weight: float32 [8192, 6], P('seq'), may hold values from 0.05 to 0.6
- segment_ids: int32 [8192], P('seq'), may hold values from 0 to 7, never falling along the last dimension, each value on 1 to 4096 neighbouring positions
Outputs:
- layer_out: bfloat16 [8192, 2048], P('seq', 'tp')
The draws below stay inside these ranges and needn't reach their ends.
Inputs may be any that keep to these rules, and one draw needn't show every extreme that they name: `expert_ids`: within the rows of one index of seq (256 aligned rows), each expert is named by at most 64 rows, a bound that some block reaches; a row names 6 different experts. `segment_ids`: ids never fall along the stream and start at 0; each prompt has 1 to 4096 tokens, one exactly 4096.
All inputs are finite; a program needn't handle non-finite values.
Results may differ from the reference program's by a relative error of at most 0.02.
Values may be sent and summed in bfloat16 or wider, within the bound.
No kernel may reach another device: no remote copies, remote signals or barrier semaphores. Data moves between devices by JAX's collectives and lax.ppermute only.
A program may use at most 192 MiB of HBM per device.

```python
import math
from functools import reduce
import jax
import jax.numpy as jnp
import numpy as np
from jax import lax

D = 2048
HEADS = 16
NOPE = 128
ROPE = 64
VDIM = 128
LATENT = 512
FE = 1408
SHARED_FF = 2816
TOPK = 6
TOK_DEV = 256
TOKENS = 8192
MAXLEN = 4096
SEGS = 8
EXPERTS = 32
CAP = 64
N_SEQ = 32
N_TP = 4


def draw_tokens(key, part):
    sample = jnp.clip(jax.random.normal(key, (TOKENS, D), jnp.float32), -6.0, 6.0)
    return sample.astype(jnp.bfloat16)


def draw_q_weight(key, part):
    sample = jnp.clip(jax.random.normal(key, (D, HEADS * (NOPE + ROPE)), jnp.float32), -6.0, 6.0) * D ** (-0.5)
    return sample.astype(jnp.bfloat16)


def draw_kva_weight(key, part):
    sample = jnp.clip(jax.random.normal(key, (D, LATENT + ROPE), jnp.float32), -6.0, 6.0) * D ** (-0.5)
    return sample.astype(jnp.bfloat16)


def steps_of(own_key, shape, cuts, least, largest):
    loudness, own = 1.0, jax.random.fold_in(own_key, 6)
    for dim, blocks in cuts:
        draws = jnp.exp(jax.random.uniform(jax.random.fold_in(own, dim), (blocks,), jnp.float32, least / len(cuts), largest / len(cuts)))
        loudness = loudness * jnp.repeat(draws, shape[dim] // blocks).reshape([-1 if axis == dim else 1 for axis in range(len(shape))])
    return loudness


def split_up(number_of, total, most, slope):
    portions = [(1 << 20) // math.isqrt(standing ** slope) + 1 for standing in range(2, number_of + 1)]
    rest, given = total - most - (number_of - 1), [1] * (number_of - 1)
    while rest > 0:
        movable = [i for i in range(number_of - 1) if given[i] < most]
        mass, remaining = sum([portions[i] for i in movable]), rest
        for i in movable:
            extra = min(most - given[i], max(1, remaining * portions[i] // mass), rest)
            given[i] = given[i] + extra
            rest = rest - extra
    return np.array([most] + given)


def ragged(rng, number_of, total, bound, slope):
    if number_of == 2:
        one = jax.random.randint(rng, (), max(1, total - bound), min(bound, total - 1) + 1)
        return jnp.stack([one, total - one])
    lengths = jnp.asarray(split_up(number_of, total, bound, slope), jnp.int32)
    couples = (number_of - 1) // 2
    giver, sink = lengths[1:1 + 2 * couples:2], lengths[2:2 + 2 * couples:2]
    margin = jnp.minimum(giver - 1, bound - sink)
    passed = jax.random.randint(jax.random.fold_in(rng, 1), (couples,), 0, 1 << 20) % (margin + 1)
    lengths = lengths.at[1:1 + 2 * couples:2].set(giver - passed).at[2:2 + 2 * couples:2].set(sink + passed)
    return lengths[jax.random.permutation(jax.random.fold_in(rng, 2), number_of)]


def routed_block(stream_key, own, number, rows, count, top, limit, skew):
    sequence = jax.random.permutation(stream_key, count)
    crowded, common = shares(count, rows * top, limit, skew, True), shares(count, rows * top, limit, skew, False)
    places = jnp.arange(count)

    def named(sizes, offset_by):
        used = int((sizes > 0).sum())
        fixed = max(1, used // 4)
        passed = fixed + (places - fixed + offset_by * (used - fixed)) % max(1, count - fixed)
        return jnp.zeros((count,), jnp.int32).at[sequence[jnp.where(places < fixed, places, passed)]].set(jnp.asarray(sizes, jnp.int32))

    sizes = jnp.where(number % 4 == 0, named(crowded, number // 4), named(common, number - number // 4 - 1))
    mixed = jax.random.permutation(jax.random.fold_in(own, 3), count)
    giver, receiver = mixed[0:count // 2 * 2:2], mixed[1:count // 2 * 2:2]
    slack = jnp.minimum(sizes[giver] - 1, limit - sizes[receiver]) // 2
    slack = jnp.where((giver == sequence[0]) | (receiver == sequence[0]) | (sizes[receiver] == 0), 0, jnp.maximum(slack, 0))
    passed = jax.random.randint(jax.random.fold_in(own, 4), (count // 2,), 0, 1 << 20) % (slack + 1)
    sizes = sizes.at[giver].add(-passed).at[receiver].add(passed)
    items = jnp.searchsorted(jnp.cumsum(sizes), jnp.arange(rows * top), side="right").astype(jnp.int32)
    listing = items.reshape(top, rows).T
    listing = listing[jax.random.permutation(jax.random.fold_in(own, 1), rows)]
    offset_by = jax.random.randint(jax.random.fold_in(own, 2), (rows, 1), 0, top)
    return jnp.take_along_axis(listing, (jnp.arange(top)[None, :] + offset_by) % top, axis=1)


def shares(number_of, total, most, skew, full):
    weights = [(1 << 20) // math.isqrt(standing ** skew) + 1 for standing in range(1, number_of + 1)]
    largest = most if full else min(most, max(-(-total // number_of), total * weights[0] // sum(weights)))
    least = 1 if total - largest >= number_of - 1 else 0
    counts, rest = [largest] + [least] * (number_of - 1), total - largest - least * (number_of - 1)
    while rest > 0:
        free = [i for i in range(1, number_of) if counts[i] < largest] or [i for i in range(1, number_of) if counts[i] < most]
        whole, budget = sum([weights[i] for i in free]), rest
        for i in free:
            extra = min(most - counts[i], max(1, budget * weights[i] // whole), rest)
            counts[i] = counts[i] + extra
            rest = rest - extra
    return np.array(counts)


def gaussian(rng, extent, scale, most, split=(), kind=jnp.bfloat16):
    level = steps_of(rng, extent, split, -0.22, 0.18) if split else 1.0
    entries = jax.random.normal(rng, extent, jnp.float32) * scale * level
    return jnp.minimum(jnp.maximum(entries, -most), most).astype(kind)


def setup_inputs(seed: int = 0) -> dict:
    key_list = jax.random.split(jax.random.key(seed), 16)
    tokens = draw_tokens(jax.random.fold_in(key_list[15], 71), 0)
    attn_gain = jnp.clip(1.0 + 0.15 * jax.random.normal(key_list[1], (D,), jnp.float32), 0.25, 1.75)
    q_weight = draw_q_weight(jax.random.fold_in(key_list[15], 71), 0)
    kva_weight = draw_kva_weight(jax.random.fold_in(key_list[15], 71), 0)
    kv_gain = jnp.clip(1.0 + 0.15 * jax.random.normal(key_list[4], (LATENT,), jnp.float32), 0.25, 1.75)
    kvb_weight = gaussian(key_list[5], (LATENT, HEADS * (NOPE + VDIM)), LATENT ** -0.5, 0.25, ((1, 4),))
    o_weight = gaussian(key_list[6], (HEADS * VDIM, D), (HEADS * VDIM) ** -0.5, 0.125, ((0, 4),))
    ffn_gain = jnp.clip(1.0 + 0.15 * jax.random.normal(key_list[7], (D,), jnp.float32), 0.25, 1.75)
    shared_gate_up = gaussian(key_list[8], (2, D, SHARED_FF), D ** -0.5, 0.125, ((2, 4),))
    shared_down = gaussian(key_list[9], (SHARED_FF, D), SHARED_FF ** -0.5, 0.109375, ((0, 4),))
    expert_gate_up = gaussian(key_list[10], (EXPERTS, 2, D, FE), D ** -0.5, 0.125, ((0, 32), (3, 4)))
    expert_down = gaussian(key_list[11], (EXPERTS, FE, D), FE ** -0.5, 0.15625, ((0, 32), (1, 4)))
    expert_ids_keys = jax.random.split(jax.random.fold_in(key_list[12], 1), TOKENS // TOK_DEV)
    expert_ids_turns = jax.random.permutation(jax.random.fold_in(key_list[12], 3), TOKENS // TOK_DEV)
    expert_ids = jax.vmap(lambda own, number: routed_block(jax.random.fold_in(key_list[12], 2), own, number, TOK_DEV, EXPERTS, TOPK, CAP, 2))(expert_ids_keys, expert_ids_turns).reshape((TOKENS, TOPK))
    route_weight = jnp.clip(jnp.exp(math.log(0.6) - 2.4849067 * jax.random.uniform(key_list[13], (TOKENS, TOPK), jnp.float32) ** steps_of(key_list[13], (TOKENS, TOPK), ((0, 32),), -0.2, 0.2)), 0.05, 0.6)
    segment_ids = jnp.searchsorted(jnp.cumsum(ragged(key_list[14], SEGS, TOKENS, MAXLEN, 2)), jnp.arange(TOKENS), side="right").astype(jnp.int32)
    return dict(tokens=tokens, attn_gain=attn_gain, q_weight=q_weight, kva_weight=kva_weight, kv_gain=kv_gain, kvb_weight=kvb_weight, o_weight=o_weight, ffn_gain=ffn_gain, shared_gate_up=shared_gate_up, shared_down=shared_down, expert_gate_up=expert_gate_up, expert_down=expert_down, expert_ids=expert_ids, route_weight=route_weight, segment_ids=segment_ids)


epsilon = 1e-06

def rms_norm(values, gain):
    return values * lax.rsqrt(lax.optimization_barrier(jnp.mean(values * values, axis=-1, keepdims=True)) + epsilon) * gain

def rotate(values, positions):
    half_width = values.shape[-1] // 2
    frequency = 10000.0 ** (-(jnp.arange(half_width).astype(jnp.float32) * 2.0 / values.shape[-1]))
    angles = positions[..., None] * frequency
    first_half = values[..., :half_width]
    second_half = values[..., half_width:]
    return jnp.concatenate([first_half * jnp.cos(angles) - second_half * jnp.sin(angles), second_half * jnp.cos(angles) + first_half * jnp.sin(angles)], axis=-1)

def add_pair(left_term, right_term):
    return left_term + right_term

def reference(tokens, attn_gain, q_weight, kva_weight, kv_gain, kvb_weight, o_weight, ffn_gain, shared_gate_up, shared_down, expert_gate_up, expert_down, expert_ids, route_weight, segment_ids):
    inputs = tokens.astype(jnp.float32)
    normed = rms_norm(inputs, attn_gain).astype(jnp.bfloat16)
    positions = jnp.arange(TOKENS).astype(jnp.float32)
    queries = jnp.dot(normed, q_weight, preferred_element_type=jnp.float32).reshape(TOKENS, HEADS, NOPE + ROPE)
    queries = jnp.concatenate([queries[..., :NOPE], rotate(queries[..., NOPE:], positions[:, None])], axis=-1).astype(jnp.bfloat16)
    compressed = jnp.dot(normed, kva_weight, preferred_element_type=jnp.float32)
    latent = rms_norm(compressed[:, :LATENT], kv_gain).astype(jnp.bfloat16)
    key_rope = rotate(compressed[:, LATENT:], positions).astype(jnp.bfloat16)
    expanded = jnp.dot(latent, kvb_weight, preferred_element_type=jnp.float32).astype(jnp.bfloat16)
    expanded = expanded.reshape(TOKENS, HEADS, NOPE + VDIM)
    key_nope = expanded[..., :NOPE].astype(jnp.float32)
    values_all = expanded[..., NOPE:].astype(jnp.float32)
    query_float = queries.astype(jnp.float32)
    rope_float = key_rope.astype(jnp.float32)
    scale = (NOPE + ROPE) ** (-0.5)
    block_rows = min(512, TOKENS)
    index_all = jnp.arange(TOKENS, dtype=jnp.int32)

    def attend_block(block):
        begin = (block * block_rows).astype(jnp.int32)
        query_block = lax.dynamic_slice_in_dim(query_float, begin, block_rows, 0)
        query_ids = lax.dynamic_slice_in_dim(segment_ids, begin, block_rows, 0)
        query_index = begin + jnp.arange(block_rows, dtype=jnp.int32)
        scores = jnp.einsum('qhc,khc->hqk', query_block[..., :NOPE], key_nope)
        scores = (scores + jnp.einsum('qhr,kr->hqk', query_block[..., NOPE:], rope_float)) * scale
        allowed = (segment_ids[None, :] == query_ids[:, None]) & (index_all[None, :] <= query_index[:, None])
        top_score = lax.optimization_barrier(jnp.max(jnp.where(allowed[None], scores, -1e+30), axis=-1, keepdims=True))
        weights = jnp.where(allowed[None], jnp.exp(scores - top_score), 0.0)
        weights = weights / lax.optimization_barrier(jnp.sum(weights, axis=-1, keepdims=True))
        weights = lax.optimization_barrier(weights.astype(jnp.bfloat16)).astype(jnp.float32)
        mixed = jnp.einsum('hqk,khc->qhc', weights, values_all)
        return mixed.astype(jnp.bfloat16).reshape(block_rows, HEADS * VDIM)
    head_out = lax.map(attend_block, jnp.arange(TOKENS // block_rows, dtype=jnp.int32)).reshape(TOKENS, HEADS * VDIM)
    hidden = inputs + jnp.dot(head_out, o_weight, preferred_element_type=jnp.float32)
    mixed_in = rms_norm(hidden, ffn_gain).astype(jnp.bfloat16)
    shared_act = (jax.nn.silu(jnp.dot(mixed_in, shared_gate_up[0], preferred_element_type=jnp.float32)) * jnp.dot(mixed_in, shared_gate_up[1], preferred_element_type=jnp.float32)).astype(jnp.bfloat16)
    shared_out = jnp.dot(shared_act, shared_down, preferred_element_type=jnp.float32)
    flat_ids = expert_ids.reshape(-1)
    flat_weight = route_weight.reshape(-1)
    part_width = FE // N_TP
    slot_total = CAP * N_SEQ

    def per_expert(routed, expert_inputs):
        expert, gate_up, down = expert_inputs
        chosen = flat_ids == expert
        picks = jnp.nonzero(chosen, size=slot_total, fill_value=0)[0].astype(jnp.int32)
        valid = jnp.arange(slot_total, dtype=jnp.int32) < jnp.sum(chosen.astype(jnp.int32))
        token_rows = picks // TOPK
        rows_in = mixed_in[token_rows]
        activated = (jax.nn.silu(jnp.dot(rows_in, gate_up[0], preferred_element_type=jnp.float32)) * jnp.dot(rows_in, gate_up[1], preferred_element_type=jnp.float32)).astype(jnp.bfloat16)
        pieces = []
        for group in range(N_TP):
            partial_value = jnp.dot(activated[:, group * part_width:(group + 1) * part_width], down[group * part_width:(group + 1) * part_width], preferred_element_type=jnp.float32)
            pieces.append(lax.optimization_barrier(partial_value.astype(jnp.bfloat16)).astype(jnp.float32))
        output = lax.optimization_barrier(reduce(add_pair, pieces).astype(jnp.bfloat16)).astype(jnp.float32)
        scaled = jnp.where(valid, flat_weight[picks], 0.0)[:, None] * output
        return (routed.at[token_rows].add(scaled), None)
    routed = lax.scan(per_expert, jnp.zeros((TOKENS, D), jnp.float32), (jnp.arange(EXPERTS, dtype=jnp.int32), expert_gate_up, expert_down))[0]
    return (hidden + shared_out + routed).astype(jnp.bfloat16)
```

```python
import jax
import jax.numpy as jnp
from jax import lax
from jax.sharding import PartitionSpec as P

D = 2048
NOPE = 128
ROPE = 64
VDIM = 128
LATENT = 512
TOPK = 6


epsilon = 1e-06


def from_behind(block, axis, distance):
    devices = range(lax.axis_size(axis))
    route = [(i - distance, i) for i in devices if i - distance in devices]
    return lax.ppermute(block, axis, route)


def rms_norm(values, gain):
    return values * lax.rsqrt(jnp.mean(values * values, axis=-1, keepdims=True) + epsilon) * gain


def rotate(values, positions):
    half_width = values.shape[-1] // 2
    frequency = 10000.0 ** (-(jnp.arange(half_width).astype(jnp.float32) * 2.0 / values.shape[-1]))
    angles = positions[..., None] * frequency
    first_half = values[..., :half_width]
    second_half = values[..., half_width:]
    return jnp.concatenate(
        [
            first_half * jnp.cos(angles) - second_half * jnp.sin(angles),
            second_half * jnp.cos(angles) + first_half * jnp.sin(angles),
        ],
        axis=-1,
    )


def local(
    tokens,
    attn_gain,
    q_weight,
    kva_weight,
    kv_gain,
    kvb_weight,
    o_weight,
    ffn_gain,
    shared_gate_up,
    shared_down,
    expert_gate_up,
    expert_down,
    expert_ids,
    route_weight,
    segment_ids,
):
    tok_rows = tokens.shape[0]
    local_heads = q_weight.shape[1] // (NOPE + ROPE)
    first_row = lax.axis_index("seq") * tok_rows
    row_index = first_row + jnp.arange(tok_rows, dtype=jnp.int32)
    positions = row_index.astype(jnp.float32)
    inputs = tokens.astype(jnp.float32)
    normed = rms_norm(inputs, attn_gain).astype(jnp.bfloat16)
    queries = jnp.dot(normed, q_weight, preferred_element_type=jnp.float32).reshape(
        tok_rows, local_heads, NOPE + ROPE
    )
    queries = jnp.concatenate(
        [queries[..., :NOPE], rotate(queries[..., NOPE:], positions[:, None])], axis=-1
    ).astype(jnp.bfloat16)
    query_nope = queries[..., :NOPE]
    query_rope = queries[..., NOPE:]
    compressed = jnp.dot(normed, kva_weight, preferred_element_type=jnp.float32)
    latent = rms_norm(compressed[:, :LATENT], kv_gain).astype(jnp.bfloat16)
    key_rope = rotate(compressed[:, LATENT:], positions).astype(jnp.bfloat16)
    key_block = jnp.concatenate([latent, key_rope], axis=1)
    scale = (NOPE + ROPE) ** (-0.5)
    total_rows = lax.axis_size("seq") * tok_rows
    longest = min(4096, total_rows // 2)
    hop_count = (longest + tok_rows - 2) // tok_rows
    blocks = [key_block]
    block_ids = [segment_ids]
    for distance in range(1, hop_count + 1):
        moved_block, moved_ids = from_behind((key_block, segment_ids), "seq", distance)
        blocks.append(moved_block)
        block_ids.append(moved_ids)
    keys = jnp.concatenate(blocks, axis=0)
    key_ids = jnp.concatenate(block_ids, axis=0)
    key_index = jnp.concatenate(
        [first_row - d * tok_rows + jnp.arange(tok_rows, dtype=jnp.int32) for d in range(hop_count + 1)]
    )
    expanded = (
        jnp.dot(keys[:, :LATENT], kvb_weight, preferred_element_type=jnp.float32)
        .astype(jnp.bfloat16)
        .reshape(keys.shape[0], local_heads, NOPE + VDIM)
    )
    scores = jnp.einsum(
        "qhc,khc->hqk", query_nope, expanded[..., :NOPE], preferred_element_type=jnp.float32
    )
    scores = scores + jnp.einsum(
        "qhr,kr->hqk", query_rope, keys[:, LATENT:], preferred_element_type=jnp.float32
    )
    scores = scores * scale
    allowed = (
        (key_ids[None, :] == segment_ids[:, None])
        & (key_index[None, :] <= row_index[:, None])
        & (key_index[None, :] >= 0)
    )
    top = jnp.max(jnp.where(allowed[None], scores, -1e30), axis=-1, keepdims=True)
    weights = jnp.where(allowed[None], jnp.exp(scores - top), 0.0)
    weights = (weights / jnp.sum(weights, axis=-1, keepdims=True)).astype(jnp.bfloat16)
    head_out = (
        jnp.einsum("hqk,khc->qhc", weights, expanded[..., NOPE:], preferred_element_type=jnp.float32)
        .astype(jnp.bfloat16)
        .reshape(tok_rows, local_heads * VDIM)
    )
    attn_part = jnp.dot(head_out, o_weight, preferred_element_type=jnp.float32)
    hidden = inputs + lax.psum(attn_part.astype(jnp.bfloat16), "tp").astype(jnp.float32)
    mixed_in = rms_norm(hidden, ffn_gain).astype(jnp.bfloat16)
    shared_act = (
        jax.nn.silu(jnp.dot(mixed_in, shared_gate_up[0], preferred_element_type=jnp.float32))
        * jnp.dot(mixed_in, shared_gate_up[1], preferred_element_type=jnp.float32)
    ).astype(jnp.bfloat16)
    shared_part = jnp.dot(shared_act, shared_down, preferred_element_type=jnp.float32)
    tp_count = lax.axis_size("tp")
    tp_rank = lax.axis_index("tp")
    share = D // tp_count
    experts = lax.axis_size("seq") * expert_gate_up.shape[0]
    capacity = min(tok_rows, tok_rows * TOPK * 4 // (3 * experts))
    choice_ids = expert_ids.reshape(-1)
    choice_count = choice_ids.shape[0]
    order = jnp.arange(choice_count, dtype=jnp.int32)
    earlier_same = (choice_ids[None, :] == choice_ids[:, None]) & (order[None, :] < order[:, None])
    slot_index = jnp.sum(earlier_same.astype(jnp.int32), axis=1)
    destination = choice_ids * capacity + slot_index
    source_row = order // TOPK
    out_width = mixed_in.shape[1]
    slot_source = jnp.zeros((experts * capacity,), jnp.int32).at[destination].set(source_row)
    buffer = mixed_in[slot_source]
    buffer = buffer.reshape(experts, capacity, out_width)
    gate_weight = expert_gate_up[0, 0]
    up_weight = expert_gate_up[0, 1]
    down_weight = expert_down[0]
    arrived = lax.all_to_all(buffer, "seq", split_axis=0, concat_axis=0, tiled=True)
    sources = arrived.shape[0]
    slot_count = arrived.shape[1]
    flat_rows = arrived.reshape(sources * slot_count, D)
    activated = (
        jax.nn.silu(jnp.dot(flat_rows, gate_weight, preferred_element_type=jnp.float32))
        * jnp.dot(flat_rows, up_weight, preferred_element_type=jnp.float32)
    ).astype(jnp.bfloat16)
    produced = jnp.dot(activated, down_weight, preferred_element_type=jnp.float32).reshape(
        sources, slot_count, D
    )
    reduced = lax.psum_scatter(produced.astype(jnp.bfloat16), "tp", scatter_dimension=2, tiled=True)
    returned = lax.all_to_all(reduced, "seq", split_axis=0, concat_axis=0, tiled=True)
    picked = returned.reshape(experts * capacity, share)[destination].astype(jnp.float32)
    picked = picked * route_weight.reshape(-1)[:, None]
    routed = jnp.sum(picked.reshape(tok_rows, TOPK, share), axis=1)
    shared_cols = lax.psum_scatter(
        shared_part.astype(jnp.bfloat16), "tp", scatter_dimension=1, tiled=True
    ).astype(jnp.float32)
    hidden_cols = lax.dynamic_slice_in_dim(hidden, tp_rank * share, share, 1)
    return (hidden_cols + shared_cols + routed).astype(jnp.bfloat16)


def solution(mesh):
    placed = (
        P("seq", None),
        P(),
        P(None, "tp"),
        P(),
        P(),
        P(None, "tp"),
        P("tp", None),
        P(),
        P(None, None, "tp"),
        P("tp", None),
        P("seq", None, None, "tp"),
        P("seq", "tp", None),
        P("seq", None),
        P("seq", None),
        P("seq"),
    )
    return jax.shard_map(
        local, mesh=mesh, in_specs=placed, out_specs=P("seq", "tp"), check_vma=False
    )
```

```python
import jax
import jax.numpy as jnp
from jax import lax
from jax.sharding import PartitionSpec as P

D = 2048
NOPE = 128
ROPE = 64
VDIM = 128
LATENT = 512
TOPK = 6
SEGS = 8


epsilon = 1e-06


def from_behind(block, axis, distance):
    devices = range(lax.axis_size(axis))
    route = [(i - distance, i) for i in devices if i - distance in devices]
    return lax.ppermute(block, axis, route)


def around(block, axis, distance):
    count = lax.axis_size(axis)
    return lax.ppermute(block, axis, [(i, (i + distance) % count) for i in range(count)])


def rms_norm(values, gain):
    return values * lax.rsqrt(jnp.mean(values * values, axis=-1, keepdims=True) + epsilon) * gain


def rotate(values, positions):
    half_width = values.shape[-1] // 2
    frequency = 10000.0 ** (-(jnp.arange(half_width).astype(jnp.float32) * 2.0 / values.shape[-1]))
    angles = positions[..., None] * frequency
    first_half = values[..., :half_width]
    second_half = values[..., half_width:]
    return jnp.concatenate(
        [
            first_half * jnp.cos(angles) - second_half * jnp.sin(angles),
            second_half * jnp.cos(angles) + first_half * jnp.sin(angles),
        ],
        axis=-1,
    )


def local(
    tokens,
    attn_gain,
    q_weight,
    kva_weight,
    kv_gain,
    kvb_weight,
    o_weight,
    ffn_gain,
    shared_gate_up,
    shared_down,
    expert_gate_up,
    expert_down,
    expert_ids,
    route_weight,
    segment_ids,
):
    tok_rows = tokens.shape[0]
    local_heads = q_weight.shape[1] // (NOPE + ROPE)
    first_row = lax.axis_index("seq") * tok_rows
    row_index = first_row + jnp.arange(tok_rows, dtype=jnp.int32)
    positions = row_index.astype(jnp.float32)
    inputs = tokens.astype(jnp.float32)
    normed = rms_norm(inputs, attn_gain).astype(jnp.bfloat16)
    queries = jnp.dot(normed, q_weight, preferred_element_type=jnp.float32).reshape(
        tok_rows, local_heads, NOPE + ROPE
    )
    queries = jnp.concatenate(
        [queries[..., :NOPE], rotate(queries[..., NOPE:], positions[:, None])], axis=-1
    ).astype(jnp.bfloat16)
    query_nope = queries[..., :NOPE]
    query_rope = queries[..., NOPE:]
    compressed = jnp.dot(normed, kva_weight, preferred_element_type=jnp.float32)
    latent = rms_norm(compressed[:, :LATENT], kv_gain).astype(jnp.bfloat16)
    key_rope = rotate(compressed[:, LATENT:], positions).astype(jnp.bfloat16)
    key_block = jnp.concatenate([latent, key_rope], axis=1)
    scale = (NOPE + ROPE) ** (-0.5)
    segs = SEGS
    seg_counts = lax.psum(
        jnp.sum((segment_ids[:, None] == jnp.arange(segs, dtype=jnp.int32)[None, :]).astype(jnp.int32), axis=0),
        "seq",
    )
    seg_start = jnp.cumsum(seg_counts) - seg_counts
    query_start = seg_start[segment_ids]
    total_rows = lax.axis_size("seq") * tok_rows
    longest = min(4096, total_rows // 2)
    hop_count = (longest + tok_rows - 2) // tok_rows
    group = 4
    near = [from_behind(key_block, "seq", d) for d in range(group - 1, 0, -1)]
    grouped = jnp.concatenate(near + [key_block], axis=0)
    far_groups = hop_count // group
    far = [from_behind(grouped, "seq", group * m) for m in range(far_groups - 1, 0, -1)]
    singles = [from_behind(key_block, "seq", d) for d in range(hop_count, group * far_groups - 1, -1)]
    keys = jnp.concatenate(singles + far + [grouped], axis=0)
    key_count = keys.shape[0]
    key_index = first_row + tok_rows - key_count + jnp.arange(key_count, dtype=jnp.int32)
    expanded = jnp.einsum(
        "nl,lhc->hnc",
        keys[:, :LATENT],
        kvb_weight.reshape(LATENT, local_heads, NOPE + VDIM),
        preferred_element_type=jnp.float32,
    ).astype(jnp.bfloat16)
    key_full = jnp.concatenate(
        [expanded[..., :NOPE], jnp.broadcast_to(keys[None, :, LATENT:], (local_heads, key_count, ROPE))],
        axis=-1,
    )
    scores = jnp.einsum(
        "qhc,hkc->hqk", queries, key_full, preferred_element_type=jnp.float32
    )
    scores = scores * scale
    allowed = (key_index[None, :] >= query_start[:, None]) & (key_index[None, :] <= row_index[:, None])
    top = jnp.max(jnp.where(allowed[None], scores, -1e30), axis=-1, keepdims=True)
    weights = jnp.where(allowed[None], jnp.exp(scores - top), 0.0)
    weights = (weights / jnp.sum(weights, axis=-1, keepdims=True)).astype(jnp.bfloat16)
    head_out = (
        jnp.einsum("hqk,hkc->qhc", weights, expanded[..., NOPE:], preferred_element_type=jnp.float32)
        .astype(jnp.bfloat16)
        .reshape(tok_rows, local_heads * VDIM)
    )
    tp_count = lax.axis_size("tp")
    head_parts = [head_out] + [around(head_out, "tp", d) for d in range(1, tp_count)]
    o_parts = [o_weight] + [around(o_weight, "tp", d) for d in range(1, tp_count)]
    hidden = inputs + jnp.dot(
        jnp.concatenate(head_parts, axis=1),
        jnp.concatenate(o_parts, axis=0),
        preferred_element_type=jnp.float32,
    )
    mixed_in = rms_norm(hidden, ffn_gain).astype(jnp.bfloat16)
    shared_act = (
        jax.nn.silu(jnp.dot(mixed_in, shared_gate_up[0], preferred_element_type=jnp.float32))
        * jnp.dot(mixed_in, shared_gate_up[1], preferred_element_type=jnp.float32)
    ).astype(jnp.bfloat16)
    shared_part = jnp.dot(shared_act, shared_down, preferred_element_type=jnp.float32)
    tp_rank = lax.axis_index("tp")
    share = D // tp_count
    experts = lax.axis_size("seq") * expert_gate_up.shape[0]
    capacity = min(tok_rows, tok_rows * TOPK * 4 // (3 * experts))
    choice_ids = expert_ids.reshape(-1)
    choice_count = choice_ids.shape[0]
    order = jnp.arange(choice_count, dtype=jnp.int32)
    earlier_same = (choice_ids[None, :] == choice_ids[:, None]) & (order[None, :] < order[:, None])
    slot_index = jnp.sum(earlier_same.astype(jnp.int32), axis=1)
    destination = choice_ids * capacity + slot_index
    source_row = order // TOPK
    out_width = mixed_in.shape[1]
    slot_source = jnp.zeros((experts * capacity,), jnp.int32).at[destination].set(source_row)
    buffer = mixed_in[slot_source]
    buffer = buffer.reshape(experts, capacity, out_width)
    gate_weight = expert_gate_up[0, 0]
    up_weight = expert_gate_up[0, 1]
    down_weight = expert_down[0]
    arrived = lax.all_to_all(buffer, "seq", split_axis=0, concat_axis=0, tiled=True)
    sources = arrived.shape[0]
    slot_count = arrived.shape[1]
    flat_rows = arrived.reshape(sources * slot_count, D)
    activated = (
        jax.nn.silu(jnp.dot(flat_rows, gate_weight, preferred_element_type=jnp.float32))
        * jnp.dot(flat_rows, up_weight, preferred_element_type=jnp.float32)
    ).astype(jnp.bfloat16)
    produced = jnp.dot(activated, down_weight, preferred_element_type=jnp.float32).reshape(
        sources, slot_count, D
    )
    reduced = lax.psum_scatter(produced.astype(jnp.bfloat16), "tp", scatter_dimension=2, tiled=True)
    returned = lax.all_to_all(reduced, "seq", split_axis=0, concat_axis=0, tiled=True)
    picked = returned.reshape(experts * capacity, share)[destination].astype(jnp.float32)
    picked = picked * route_weight.reshape(-1)[:, None]
    routed = jnp.sum(picked.reshape(tok_rows, TOPK, share), axis=1)
    shared_cols = lax.psum_scatter(
        shared_part.astype(jnp.bfloat16), "tp", scatter_dimension=1, tiled=True
    ).astype(jnp.float32)
    hidden_cols = lax.dynamic_slice_in_dim(hidden, tp_rank * share, share, 1)
    return (hidden_cols + shared_cols + routed).astype(jnp.bfloat16)


def solution(mesh):
    placed = (
        P("seq", None),
        P(),
        P(None, "tp"),
        P(),
        P(),
        P(None, "tp"),
        P("tp", None),
        P(),
        P(None, None, "tp"),
        P("tp", None),
        P("seq", None, None, "tp"),
        P("seq", "tp", None),
        P("seq", None),
        P("seq", None),
        P("seq"),
    )
    return jax.shard_map(
        local, mesh=mesh, in_specs=placed, out_specs=P("seq", "tp"), check_vma=False
    )
```

```python
import jax
import jax.numpy as jnp
from jax import lax
from jax.sharding import PartitionSpec as P

D = 2048
NOPE = 128
ROPE = 64
VDIM = 128
LATENT = 512
TOPK = 6
SEGS = 8


epsilon = 1e-06


def from_behind(block, axis, distance):
    devices = range(lax.axis_size(axis))
    route = [(i - distance, i) for i in devices if i - distance in devices]
    return lax.ppermute(block, axis, route)


def around(block, axis, distance):
    count = lax.axis_size(axis)
    return lax.ppermute(block, axis, [(i, (i + distance) % count) for i in range(count)])


def rms_norm(values, gain):
    return values * lax.rsqrt(jnp.mean(values * values, axis=-1, keepdims=True) + epsilon) * gain


def rotate(values, positions):
    half_width = values.shape[-1] // 2
    frequency = 10000.0 ** (-(jnp.arange(half_width).astype(jnp.float32) * 2.0 / values.shape[-1]))
    angles = positions[..., None] * frequency
    first_half = values[..., :half_width]
    second_half = values[..., half_width:]
    return jnp.concatenate(
        [
            first_half * jnp.cos(angles) - second_half * jnp.sin(angles),
            second_half * jnp.cos(angles) + first_half * jnp.sin(angles),
        ],
        axis=-1,
    )


def local(
    tokens,
    attn_gain,
    q_weight,
    kva_weight,
    kv_gain,
    kvb_weight,
    o_weight,
    ffn_gain,
    shared_gate_up,
    shared_down,
    expert_gate_up,
    expert_down,
    expert_ids,
    route_weight,
    segment_ids,
):
    tok_rows = tokens.shape[0]
    local_heads = q_weight.shape[1] // (NOPE + ROPE)
    first_row = lax.axis_index("seq") * tok_rows
    row_index = first_row + jnp.arange(tok_rows, dtype=jnp.int32)
    positions = row_index.astype(jnp.float32)
    inputs = tokens.astype(jnp.float32)
    normed = rms_norm(inputs, attn_gain).astype(jnp.bfloat16)
    queries = jnp.dot(normed, q_weight, preferred_element_type=jnp.float32).reshape(
        tok_rows, local_heads, NOPE + ROPE
    )
    queries = jnp.concatenate(
        [queries[..., :NOPE], rotate(queries[..., NOPE:], positions[:, None])], axis=-1
    ).astype(jnp.bfloat16)
    query_nope = queries[..., :NOPE]
    query_rope = queries[..., NOPE:]
    compressed = jnp.dot(normed, kva_weight, preferred_element_type=jnp.float32)
    latent = rms_norm(compressed[:, :LATENT], kv_gain).astype(jnp.bfloat16)
    key_rope = rotate(compressed[:, LATENT:], positions).astype(jnp.bfloat16)
    key_block = jnp.concatenate([latent, key_rope], axis=1)
    scale = (NOPE + ROPE) ** (-0.5)
    segs = SEGS
    seg_counts = lax.psum(
        jnp.sum((segment_ids[:, None] == jnp.arange(segs, dtype=jnp.int32)[None, :]).astype(jnp.int32), axis=0),
        "seq",
    )
    seg_start = jnp.cumsum(seg_counts) - seg_counts
    query_start = seg_start[segment_ids]
    total_rows = lax.axis_size("seq") * tok_rows
    longest = min(4096, total_rows // 2)
    hop_count = (longest + tok_rows - 2) // tok_rows
    group = 4
    near = [from_behind(key_block, "seq", d) for d in range(group - 1, 0, -1)]
    grouped = jnp.concatenate(near + [key_block], axis=0)
    far_groups = hop_count // group
    far = [from_behind(grouped, "seq", group * m) for m in range(far_groups - 1, 0, -1)]
    singles = [from_behind(key_block, "seq", d) for d in range(hop_count, group * far_groups - 1, -1)]
    keys = jnp.concatenate(singles + far + [grouped], axis=0)
    key_count = keys.shape[0]
    key_index = first_row + tok_rows - key_count + jnp.arange(key_count, dtype=jnp.int32)
    expanded = jnp.einsum(
        "nl,lhc->hnc",
        keys[:, :LATENT],
        kvb_weight.reshape(LATENT, local_heads, NOPE + VDIM),
        preferred_element_type=jnp.float32,
    ).astype(jnp.bfloat16)
    key_full = jnp.concatenate(
        [expanded[..., :NOPE], jnp.broadcast_to(keys[None, :, LATENT:], (local_heads, key_count, ROPE))],
        axis=-1,
    )
    scores = jnp.einsum(
        "qhc,hkc->hqk", queries, key_full, preferred_element_type=jnp.float32
    )
    scores = scores * scale
    allowed = (key_index[None, :] >= query_start[:, None]) & (key_index[None, :] <= row_index[:, None])
    top = jnp.max(jnp.where(allowed[None], scores, -1e30), axis=-1, keepdims=True)
    weights = jnp.where(allowed[None], jnp.exp(scores - top), 0.0)
    weights = (weights / jnp.sum(weights, axis=-1, keepdims=True)).astype(jnp.bfloat16)
    head_out = (
        jnp.einsum("hqk,hkc->qhc", weights, expanded[..., NOPE:], preferred_element_type=jnp.float32)
        .astype(jnp.bfloat16)
        .reshape(tok_rows, local_heads * VDIM)
    )
    tp_count = lax.axis_size("tp")
    head_parts = [head_out] + [around(head_out, "tp", d) for d in range(1, tp_count)]
    o_parts = [o_weight] + [around(o_weight, "tp", d) for d in range(1, tp_count)]
    hidden = inputs + jnp.dot(
        jnp.concatenate(head_parts, axis=1),
        jnp.concatenate(o_parts, axis=0),
        preferred_element_type=jnp.float32,
    )
    mixed_in = rms_norm(hidden, ffn_gain).astype(jnp.bfloat16)
    shared_act = (
        jax.nn.silu(jnp.dot(mixed_in, shared_gate_up[0], preferred_element_type=jnp.float32))
        * jnp.dot(mixed_in, shared_gate_up[1], preferred_element_type=jnp.float32)
    ).astype(jnp.bfloat16)
    shared_part = jnp.dot(shared_act, shared_down, preferred_element_type=jnp.float32)
    tp_rank = lax.axis_index("tp")
    tp_count = lax.axis_size("tp")
    share = D // tp_count
    experts = lax.axis_size("seq") * expert_gate_up.shape[0]
    capacity = min(tok_rows, tok_rows * TOPK * 4 // (3 * experts))
    choice_ids = expert_ids.reshape(-1)
    choice_count = choice_ids.shape[0]
    order = jnp.arange(choice_count, dtype=jnp.int32)
    earlier_same = (choice_ids[None, :] == choice_ids[:, None]) & (order[None, :] < order[:, None])
    slot_index = jnp.sum(earlier_same.astype(jnp.int32), axis=1)
    destination = choice_ids * capacity + slot_index
    source_row = order // TOPK
    out_width = mixed_in.shape[1]
    slot_source = jnp.zeros((experts * capacity,), jnp.int32).at[destination].set(source_row)
    tp_share = capacity // tp_count
    my_slots = lax.dynamic_slice_in_dim(
        slot_source.reshape(experts, capacity), tp_rank * tp_share, tp_share, 1
    )
    buffer = mixed_in[my_slots.reshape(-1)].reshape(experts, tp_share, out_width)
    hidden_part = expert_gate_up.shape[3]
    packed = jnp.concatenate(
        [expert_gate_up[0].reshape(2 * D, hidden_part), expert_down[0].T], axis=0
    )
    weight_parts = [packed] + [around(packed, "tp", d) for d in range(1, tp_count)]
    arrived = lax.all_to_all(buffer, "seq", split_axis=0, concat_axis=0, tiled=True)
    sources = arrived.shape[0]
    flat_rows = arrived.reshape(sources * tp_share, D)
    produced = None
    for part in weight_parts:
        gate_weight = part[:D]
        up_weight = part[D : 2 * D]
        down_weight_t = part[2 * D :]
        activated = (
            jax.nn.silu(jnp.dot(flat_rows, gate_weight, preferred_element_type=jnp.float32))
            * jnp.dot(flat_rows, up_weight, preferred_element_type=jnp.float32)
        ).astype(jnp.bfloat16)
        piece = lax.dot_general(
            activated, down_weight_t, (((1,), (1,)), ((), ())), preferred_element_type=jnp.float32
        ).astype(jnp.bfloat16).astype(jnp.float32)
        produced = piece if produced is None else produced + piece
    produced = produced.astype(jnp.bfloat16).reshape(sources, tp_share, D)
    returned = lax.all_to_all(produced, "seq", split_axis=0, concat_axis=0, tiled=True)
    returned = returned.reshape(experts, tp_share, tp_count, share)
    regrouped = lax.all_to_all(returned, "tp", split_axis=2, concat_axis=1, tiled=True)
    picked = regrouped.reshape(experts * capacity, share)[destination].astype(jnp.float32)
    picked = picked * route_weight.reshape(-1)[:, None]
    routed = jnp.sum(picked.reshape(tok_rows, TOPK, share), axis=1)
    shared_cols = lax.psum_scatter(
        shared_part.astype(jnp.bfloat16), "tp", scatter_dimension=1, tiled=True
    ).astype(jnp.float32)
    hidden_cols = lax.dynamic_slice_in_dim(hidden, tp_rank * share, share, 1)
    return (hidden_cols + shared_cols + routed).astype(jnp.bfloat16)


def solution(mesh):
    placed = (
        P("seq", None),
        P(),
        P(None, "tp"),
        P(),
        P(),
        P(None, "tp"),
        P("tp", None),
        P(),
        P(None, None, "tp"),
        P("tp", None),
        P("seq", None, None, "tp"),
        P("seq", "tp", None),
        P("seq", None),
        P("seq", None),
        P("seq"),
    )
    return jax.shard_map(
        local, mesh=mesh, in_specs=placed, out_specs=P("seq", "tp"), check_vma=False
    )
```

```python
import jax
import jax.numpy as jnp
from jax import lax
from jax.sharding import PartitionSpec as P

D = 2048
NOPE = 128
ROPE = 64
VDIM = 128
LATENT = 512
TOPK = 6
SEGS = 8


epsilon = 1e-06


def from_behind(block, axis, distance):
    devices = range(lax.axis_size(axis))
    route = [(i - distance, i) for i in devices if i - distance in devices]
    return lax.ppermute(block, axis, route)


def around(block, axis, distance):
    count = lax.axis_size(axis)
    return lax.ppermute(block, axis, [(i, (i + distance) % count) for i in range(count)])


def rms_norm(values, gain):
    return values * lax.rsqrt(jnp.mean(values * values, axis=-1, keepdims=True) + epsilon) * gain


def rotate(values, positions):
    half_width = values.shape[-1] // 2
    frequency = 10000.0 ** (-(jnp.arange(half_width).astype(jnp.float32) * 2.0 / values.shape[-1]))
    angles = positions[..., None] * frequency
    first_half = values[..., :half_width]
    second_half = values[..., half_width:]
    return jnp.concatenate(
        [
            first_half * jnp.cos(angles) - second_half * jnp.sin(angles),
            second_half * jnp.cos(angles) + first_half * jnp.sin(angles),
        ],
        axis=-1,
    )


def local(
    tokens,
    attn_gain,
    q_weight,
    kva_weight,
    kv_gain,
    kvb_weight,
    o_weight,
    ffn_gain,
    shared_gate_up,
    shared_down,
    expert_gate_up,
    expert_down,
    expert_ids,
    route_weight,
    segment_ids,
):
    tok_rows = tokens.shape[0]
    local_heads = q_weight.shape[1] // (NOPE + ROPE)
    first_row = lax.axis_index("seq") * tok_rows
    row_index = first_row + jnp.arange(tok_rows, dtype=jnp.int32)
    positions = row_index.astype(jnp.float32)
    inputs = tokens.astype(jnp.float32)
    normed = rms_norm(inputs, attn_gain).astype(jnp.bfloat16)
    queries = jnp.dot(normed, q_weight, preferred_element_type=jnp.float32).reshape(
        tok_rows, local_heads, NOPE + ROPE
    )
    queries = jnp.concatenate(
        [queries[..., :NOPE], rotate(queries[..., NOPE:], positions[:, None])], axis=-1
    ).astype(jnp.bfloat16)
    query_nope = queries[..., :NOPE]
    query_rope = queries[..., NOPE:]
    compressed = jnp.dot(normed, kva_weight, preferred_element_type=jnp.float32)
    latent = rms_norm(compressed[:, :LATENT], kv_gain).astype(jnp.bfloat16)
    key_rope = rotate(compressed[:, LATENT:], positions).astype(jnp.bfloat16)
    key_block = jnp.concatenate([latent, key_rope], axis=1)
    scale = (NOPE + ROPE) ** (-0.5)
    segs = SEGS
    seg_counts = lax.psum(
        jnp.sum((segment_ids[:, None] == jnp.arange(segs, dtype=jnp.int32)[None, :]).astype(jnp.int32), axis=0),
        "seq",
    )
    seg_start = jnp.cumsum(seg_counts) - seg_counts
    query_start = seg_start[segment_ids]
    total_rows = lax.axis_size("seq") * tok_rows
    longest = min(4096, total_rows // 2)
    hop_count = (longest + tok_rows - 2) // tok_rows
    group = 4
    near = [from_behind(key_block, "seq", d) for d in range(group - 1, 0, -1)]
    grouped = jnp.concatenate(near + [key_block], axis=0)
    far_groups = hop_count // group
    far = [from_behind(grouped, "seq", group * m) for m in range(far_groups - 1, 0, -1)]
    singles = [from_behind(key_block, "seq", d) for d in range(hop_count, group * far_groups - 1, -1)]
    keys = jnp.concatenate(singles + far + [grouped], axis=0)
    key_count = keys.shape[0]
    key_index = first_row + tok_rows - key_count + jnp.arange(key_count, dtype=jnp.int32)
    expanded = jnp.einsum(
        "nl,lhc->hnc",
        keys[:, :LATENT],
        kvb_weight.reshape(LATENT, local_heads, NOPE + VDIM),
        preferred_element_type=jnp.float32,
    ).astype(jnp.bfloat16)
    key_full = jnp.concatenate(
        [expanded[..., :NOPE], jnp.broadcast_to(keys[None, :, LATENT:], (local_heads, key_count, ROPE))],
        axis=-1,
    )
    scores = jnp.einsum(
        "qhc,hkc->hqk", queries, key_full, preferred_element_type=jnp.float32
    )
    scores = scores * scale
    allowed = (key_index[None, :] >= query_start[:, None]) & (key_index[None, :] <= row_index[:, None])
    top = jnp.max(jnp.where(allowed[None], scores, -1e30), axis=-1, keepdims=True)
    weights = jnp.where(allowed[None], jnp.exp(scores - top), 0.0)
    weights = (weights / jnp.sum(weights, axis=-1, keepdims=True)).astype(jnp.bfloat16)
    head_out = (
        jnp.einsum("hqk,hkc->qhc", weights, expanded[..., NOPE:], preferred_element_type=jnp.float32)
        .astype(jnp.bfloat16)
        .reshape(tok_rows, local_heads * VDIM)
    )
    tp_count = lax.axis_size("tp")
    attn_part = jnp.dot(head_out, o_weight, preferred_element_type=jnp.float32)
    hidden = inputs + lax.psum(attn_part.astype(jnp.bfloat16), "tp").astype(jnp.float32)
    mixed_in = rms_norm(hidden, ffn_gain).astype(jnp.bfloat16)
    shared_act = (
        jax.nn.silu(jnp.dot(mixed_in, shared_gate_up[0], preferred_element_type=jnp.float32))
        * jnp.dot(mixed_in, shared_gate_up[1], preferred_element_type=jnp.float32)
    ).astype(jnp.bfloat16)
    shared_part = jnp.dot(shared_act, shared_down, preferred_element_type=jnp.float32)
    tp_rank = lax.axis_index("tp")
    tp_count = lax.axis_size("tp")
    share = D // tp_count
    experts = lax.axis_size("seq") * expert_gate_up.shape[0]
    capacity = min(tok_rows, tok_rows * TOPK * 4 // (3 * experts))
    choice_ids = expert_ids.reshape(-1)
    choice_count = choice_ids.shape[0]
    order = jnp.arange(choice_count, dtype=jnp.int32)
    earlier_same = (choice_ids[None, :] == choice_ids[:, None]) & (order[None, :] < order[:, None])
    slot_index = jnp.sum(earlier_same.astype(jnp.int32), axis=1)
    destination = choice_ids * capacity + slot_index
    source_row = order // TOPK
    out_width = mixed_in.shape[1]
    slot_source = jnp.zeros((experts * capacity,), jnp.int32).at[destination].set(source_row)
    tp_share = capacity // tp_count
    my_slots = lax.dynamic_slice_in_dim(
        slot_source.reshape(experts, capacity), tp_rank * tp_share, tp_share, 1
    )
    buffer = mixed_in[my_slots.reshape(-1)].reshape(experts, tp_share, out_width)
    hidden_part = expert_gate_up.shape[3]
    packed = jnp.concatenate(
        [expert_gate_up[0].reshape(2 * D, hidden_part), expert_down[0].T], axis=0
    )
    weight_parts = [packed] + [around(packed, "tp", d) for d in range(1, tp_count)]
    arrived = lax.all_to_all(buffer, "seq", split_axis=0, concat_axis=0, tiled=True)
    sources = arrived.shape[0]
    flat_rows = arrived.reshape(sources * tp_share, D)
    produced = None
    for part in weight_parts:
        gate_weight = part[:D]
        up_weight = part[D : 2 * D]
        down_weight_t = part[2 * D :]
        activated = (
            jax.nn.silu(jnp.dot(flat_rows, gate_weight, preferred_element_type=jnp.float32))
            * jnp.dot(flat_rows, up_weight, preferred_element_type=jnp.float32)
        ).astype(jnp.bfloat16)
        piece = lax.dot_general(
            activated, down_weight_t, (((1,), (1,)), ((), ())), preferred_element_type=jnp.float32
        ).astype(jnp.bfloat16).astype(jnp.float32)
        produced = piece if produced is None else produced + piece
    produced = produced.astype(jnp.bfloat16).reshape(sources, tp_share, D)
    returned = lax.all_to_all(produced, "seq", split_axis=0, concat_axis=0, tiled=True)
    returned = returned.reshape(experts, tp_share, tp_count, share)
    regrouped = lax.all_to_all(returned, "tp", split_axis=2, concat_axis=1, tiled=True)
    picked = regrouped.reshape(experts * capacity, share)[destination].astype(jnp.float32)
    picked = picked * route_weight.reshape(-1)[:, None]
    routed = jnp.sum(picked.reshape(tok_rows, TOPK, share), axis=1)
    shared_cols = lax.psum_scatter(
        shared_part.astype(jnp.bfloat16), "tp", scatter_dimension=1, tiled=True
    ).astype(jnp.float32)
    hidden_cols = lax.dynamic_slice_in_dim(hidden, tp_rank * share, share, 1)
    return (hidden_cols + shared_cols + routed).astype(jnp.bfloat16)


def solution(mesh):
    placed = (
        P("seq", None),
        P(),
        P(None, "tp"),
        P(),
        P(),
        P(None, "tp"),
        P("tp", None),
        P(),
        P(None, None, "tp"),
        P("tp", None),
        P("seq", None, None, "tp"),
        P("seq", "tp", None),
        P("seq", None),
        P("seq", None),
        P("seq"),
    )
    return jax.shard_map(
        local, mesh=mesh, in_specs=placed, out_specs=P("seq", "tp"), check_vma=False
    )
```

```python
import jax
import jax.numpy as jnp
from jax import lax
from jax.sharding import PartitionSpec as P

D = 2048
NOPE = 128
ROPE = 64
VDIM = 128
LATENT = 512
TOPK = 6
SEGS = 8


epsilon = 1e-06


def from_behind(block, axis, distance):
    devices = range(lax.axis_size(axis))
    route = [(i - distance, i) for i in devices if i - distance in devices]
    return lax.ppermute(block, axis, route)


def around(block, axis, distance):
    count = lax.axis_size(axis)
    return lax.ppermute(block, axis, [(i, (i + distance) % count) for i in range(count)])


def rms_norm(values, gain):
    return values * lax.rsqrt(jnp.mean(values * values, axis=-1, keepdims=True) + epsilon) * gain


def rotate(values, positions):
    half_width = values.shape[-1] // 2
    frequency = 10000.0 ** (-(jnp.arange(half_width).astype(jnp.float32) * 2.0 / values.shape[-1]))
    angles = positions[..., None] * frequency
    first_half = values[..., :half_width]
    second_half = values[..., half_width:]
    return jnp.concatenate(
        [
            first_half * jnp.cos(angles) - second_half * jnp.sin(angles),
            second_half * jnp.cos(angles) + first_half * jnp.sin(angles),
        ],
        axis=-1,
    )


def local(
    tokens,
    attn_gain,
    q_weight,
    kva_weight,
    kv_gain,
    kvb_weight,
    o_weight,
    ffn_gain,
    shared_gate_up,
    shared_down,
    expert_gate_up,
    expert_down,
    expert_ids,
    route_weight,
    segment_ids,
):
    tok_rows = tokens.shape[0]
    local_heads = q_weight.shape[1] // (NOPE + ROPE)
    first_row = lax.axis_index("seq") * tok_rows
    row_index = first_row + jnp.arange(tok_rows, dtype=jnp.int32)
    positions = row_index.astype(jnp.float32)
    inputs = tokens.astype(jnp.float32)
    normed = rms_norm(inputs, attn_gain).astype(jnp.bfloat16)
    queries = jnp.dot(normed, q_weight, preferred_element_type=jnp.float32).reshape(
        tok_rows, local_heads, NOPE + ROPE
    )
    queries = jnp.concatenate(
        [queries[..., :NOPE], rotate(queries[..., NOPE:], positions[:, None])], axis=-1
    ).astype(jnp.bfloat16)
    query_nope = queries[..., :NOPE]
    query_rope = queries[..., NOPE:]
    compressed = jnp.dot(normed, kva_weight, preferred_element_type=jnp.float32)
    latent = rms_norm(compressed[:, :LATENT], kv_gain).astype(jnp.bfloat16)
    key_rope = rotate(compressed[:, LATENT:], positions).astype(jnp.bfloat16)
    key_block = jnp.concatenate([latent, key_rope], axis=1)
    scale = (NOPE + ROPE) ** (-0.5)
    segs = SEGS
    seg_counts = lax.psum(
        jnp.sum((segment_ids[:, None] == jnp.arange(segs, dtype=jnp.int32)[None, :]).astype(jnp.float32), axis=0),
        "seq",
    ).astype(jnp.int32)
    seg_start = jnp.cumsum(seg_counts) - seg_counts
    query_start = seg_start[segment_ids]
    total_rows = lax.axis_size("seq") * tok_rows
    longest = min(4096, total_rows // 2)
    hop_count = (longest + tok_rows - 2) // tok_rows
    group = 4
    near = [from_behind(key_block, "seq", d) for d in range(group - 1, 0, -1)]
    grouped = jnp.concatenate(near + [key_block], axis=0)
    far_groups = hop_count // group
    far = [from_behind(grouped, "seq", group * m) for m in range(far_groups - 1, 0, -1)]
    singles = [from_behind(key_block, "seq", d) for d in range(hop_count, group * far_groups - 1, -1)]
    keys = jnp.concatenate(singles + far + [grouped], axis=0)
    key_count = keys.shape[0]
    key_index = first_row + tok_rows - key_count + jnp.arange(key_count, dtype=jnp.int32)
    expanded = jnp.einsum(
        "nl,lhc->hnc",
        keys[:, :LATENT],
        kvb_weight.reshape(LATENT, local_heads, NOPE + VDIM),
        preferred_element_type=jnp.float32,
    ).astype(jnp.bfloat16)
    key_full = jnp.concatenate(
        [expanded[..., :NOPE], jnp.broadcast_to(keys[None, :, LATENT:], (local_heads, key_count, ROPE))],
        axis=-1,
    )
    scores = jnp.einsum(
        "qhc,hkc->hqk", queries, key_full, preferred_element_type=jnp.float32
    )
    scores = scores * scale
    allowed = (key_index[None, :] >= query_start[:, None]) & (key_index[None, :] <= row_index[:, None])
    top = jnp.max(jnp.where(allowed[None], scores, -1e30), axis=-1, keepdims=True)
    weights = jnp.where(allowed[None], jnp.exp(scores - top), 0.0)
    weights = (weights / jnp.sum(weights, axis=-1, keepdims=True)).astype(jnp.bfloat16)
    head_out = (
        jnp.einsum("hqk,hkc->qhc", weights, expanded[..., NOPE:], preferred_element_type=jnp.float32)
        .astype(jnp.bfloat16)
        .reshape(tok_rows, local_heads * VDIM)
    )
    attn_part = jnp.dot(head_out, o_weight, preferred_element_type=jnp.float32).astype(jnp.bfloat16)
    tp_rank = lax.axis_index("tp")
    tp_count = lax.axis_size("tp")
    share = D // tp_count
    summed = lax.dynamic_slice_in_dim(attn_part, tp_rank * share, share, 1).astype(jnp.float32)
    for d in range(1, tp_count):
        outgoing = lax.dynamic_slice_in_dim(attn_part, ((tp_rank + d) % tp_count) * share, share, 1)
        summed = summed + around(outgoing, "tp", d).astype(jnp.float32)
    hidden_cols = lax.dynamic_slice_in_dim(inputs, tp_rank * share, share, 1) + summed
    hidden_rolled = jnp.concatenate(
        [around(hidden_cols, "tp", d) for d in range(tp_count - 1, 0, -1)] + [hidden_cols], axis=1
    )
    hidden = jnp.roll(hidden_rolled, ((tp_rank + 1) % tp_count) * share, axis=1)
    mixed_in = rms_norm(hidden, ffn_gain).astype(jnp.bfloat16)
    shared_act = (
        jax.nn.silu(jnp.dot(mixed_in, shared_gate_up[0], preferred_element_type=jnp.float32))
        * jnp.dot(mixed_in, shared_gate_up[1], preferred_element_type=jnp.float32)
    ).astype(jnp.bfloat16)
    shared_part = jnp.dot(shared_act, shared_down, preferred_element_type=jnp.float32)
    experts = lax.axis_size("seq") * expert_gate_up.shape[0]
    capacity = min(tok_rows, tok_rows * TOPK * 4 // (3 * experts))
    choice_ids = expert_ids.reshape(-1)
    choice_count = choice_ids.shape[0]
    order = jnp.arange(choice_count, dtype=jnp.int32)
    earlier_same = (choice_ids[None, :] == choice_ids[:, None]) & (order[None, :] < order[:, None])
    slot_index = jnp.sum(earlier_same.astype(jnp.int32), axis=1)
    destination = choice_ids * capacity + slot_index
    source_row = order // TOPK
    out_width = mixed_in.shape[1]
    slot_source = jnp.zeros((experts * capacity,), jnp.int32).at[destination].set(source_row)
    tp_share = capacity // tp_count
    my_slots = lax.dynamic_slice_in_dim(
        slot_source.reshape(experts, capacity), tp_rank * tp_share, tp_share, 1
    )
    buffer = mixed_in[my_slots.reshape(-1)].reshape(experts, tp_share, out_width)
    hidden_part = expert_gate_up.shape[3]
    packed = jnp.concatenate(
        [expert_gate_up[0].reshape(2 * D, hidden_part), expert_down[0].T], axis=0
    )
    weight_parts = [packed] + [around(packed, "tp", d) for d in range(1, tp_count)]
    arrived = lax.all_to_all(buffer, "seq", split_axis=0, concat_axis=0, tiled=True)
    sources = arrived.shape[0]
    flat_rows = arrived.reshape(sources * tp_share, D)
    produced = None
    for part in weight_parts:
        gate_weight = part[:D]
        up_weight = part[D : 2 * D]
        down_weight_t = part[2 * D :]
        activated = (
            jax.nn.silu(jnp.dot(flat_rows, gate_weight, preferred_element_type=jnp.float32))
            * jnp.dot(flat_rows, up_weight, preferred_element_type=jnp.float32)
        ).astype(jnp.bfloat16)
        piece = lax.dot_general(
            activated, down_weight_t, (((1,), (1,)), ((), ())), preferred_element_type=jnp.float32
        ).astype(jnp.bfloat16).astype(jnp.float32)
        produced = piece if produced is None else produced + piece
    produced = produced.astype(jnp.bfloat16).reshape(sources, tp_share, D)
    returned = lax.all_to_all(produced, "seq", split_axis=0, concat_axis=0, tiled=True)
    returned = returned.reshape(experts, tp_share, tp_count, share)
    regrouped = lax.all_to_all(returned, "tp", split_axis=2, concat_axis=1, tiled=True)
    chosen = destination.reshape(tok_rows, TOPK)[:, :, None] == jnp.arange(
        experts * capacity, dtype=jnp.int32
    )[None, None, :]
    combine = jnp.sum(jnp.where(chosen, route_weight[:, :, None], 0.0), axis=1)
    routed = jnp.dot(
        combine,
        regrouped.reshape(experts * capacity, share).astype(jnp.float32),
        precision=lax.Precision.HIGHEST,
        preferred_element_type=jnp.float32,
    )
    shared_cols = lax.psum_scatter(
        shared_part.astype(jnp.bfloat16), "tp", scatter_dimension=1, tiled=True
    ).astype(jnp.float32)
    return (hidden_cols + shared_cols + routed).astype(jnp.bfloat16)


def solution(mesh):
    placed = (
        P("seq", None),
        P(),
        P(None, "tp"),
        P(),
        P(),
        P(None, "tp"),
        P("tp", None),
        P(),
        P(None, None, "tp"),
        P("tp", None),
        P("seq", None, None, "tp"),
        P("seq", "tp", None),
        P("seq", None),
        P("seq", None),
        P("seq"),
    )
    return jax.shard_map(
        local, mesh=mesh, in_specs=placed, out_specs=P("seq", "tp"), check_vma=False
    )
```

```python
import jax
import jax.numpy as jnp
from jax import lax
from jax.sharding import PartitionSpec as P

D = 2048
NOPE = 128
ROPE = 64
VDIM = 128
LATENT = 512
TOPK = 6


epsilon = 1e-06


def from_behind(block, axis, distance):
    devices = range(lax.axis_size(axis))
    route = [(i - distance, i) for i in devices if i - distance in devices]
    return lax.ppermute(block, axis, route)


def around(block, axis, distance):
    count = lax.axis_size(axis)
    return lax.ppermute(block, axis, [(i, (i + distance) % count) for i in range(count)])


def rms_norm(values, gain):
    return values * lax.rsqrt(jnp.mean(values * values, axis=-1, keepdims=True) + epsilon) * gain


def rotate(values, positions):
    half_width = values.shape[-1] // 2
    frequency = 10000.0 ** (-(jnp.arange(half_width).astype(jnp.float32) * 2.0 / values.shape[-1]))
    angles = positions[..., None] * frequency
    first_half = values[..., :half_width]
    second_half = values[..., half_width:]
    return jnp.concatenate(
        [
            first_half * jnp.cos(angles) - second_half * jnp.sin(angles),
            second_half * jnp.cos(angles) + first_half * jnp.sin(angles),
        ],
        axis=-1,
    )


def local(
    tokens,
    attn_gain,
    q_weight,
    kva_weight,
    kv_gain,
    kvb_weight,
    o_weight,
    ffn_gain,
    shared_gate_up,
    shared_down,
    expert_gate_up,
    expert_down,
    expert_ids,
    route_weight,
    segment_ids,
):
    tok_rows = tokens.shape[0]
    local_heads = q_weight.shape[1] // (NOPE + ROPE)
    first_row = lax.axis_index("seq") * tok_rows
    row_index = first_row + jnp.arange(tok_rows, dtype=jnp.int32)
    positions = row_index.astype(jnp.float32)
    inputs = tokens.astype(jnp.float32)
    normed = rms_norm(inputs, attn_gain).astype(jnp.bfloat16)
    queries = jnp.dot(normed, q_weight, preferred_element_type=jnp.float32).reshape(
        tok_rows, local_heads, NOPE + ROPE
    )
    queries = jnp.concatenate(
        [queries[..., :NOPE], rotate(queries[..., NOPE:], positions[:, None])], axis=-1
    ).astype(jnp.bfloat16)
    query_nope = queries[..., :NOPE]
    query_rope = queries[..., NOPE:]
    compressed = jnp.dot(normed, kva_weight, preferred_element_type=jnp.float32)
    latent = rms_norm(compressed[:, :LATENT], kv_gain).astype(jnp.bfloat16)
    key_rope = rotate(compressed[:, LATENT:], positions).astype(jnp.bfloat16)
    key_block = jnp.concatenate(
        [latent, key_rope, segment_ids.astype(jnp.bfloat16)[:, None]], axis=1
    )
    scale = (NOPE + ROPE) ** (-0.5)
    total_rows = lax.axis_size("seq") * tok_rows
    longest = min(4096, total_rows // 2)
    hop_count = (longest + tok_rows - 2) // tok_rows
    group = 4
    near = [from_behind(key_block, "seq", d) for d in range(group - 1, 0, -1)]
    grouped = jnp.concatenate(near + [key_block], axis=0)
    far_groups = hop_count // group
    far = [from_behind(grouped, "seq", group * m) for m in range(far_groups - 1, 0, -1)]
    singles = [from_behind(key_block, "seq", d) for d in range(hop_count, group * far_groups - 1, -1)]
    keys = jnp.concatenate(singles + far + [grouped], axis=0)
    key_count = keys.shape[0]
    key_index = first_row + tok_rows - key_count + jnp.arange(key_count, dtype=jnp.int32)
    expanded = jnp.einsum(
        "nl,lhc->hnc",
        keys[:, :LATENT],
        kvb_weight.reshape(LATENT, local_heads, NOPE + VDIM),
        preferred_element_type=jnp.float32,
    ).astype(jnp.bfloat16)
    key_full = jnp.concatenate(
        [expanded[..., :NOPE], jnp.broadcast_to(keys[None, :, LATENT : LATENT + ROPE], (local_heads, key_count, ROPE))],
        axis=-1,
    )
    scores = jnp.einsum(
        "qhc,hkc->hqk", queries, key_full, preferred_element_type=jnp.float32
    )
    scores = scores * scale
    key_ids = keys[:, LATENT + ROPE].astype(jnp.int32)
    allowed = (
        (key_ids[None, :] == segment_ids[:, None])
        & (key_index[None, :] <= row_index[:, None])
        & (key_index[None, :] >= 0)
    )
    top = jnp.max(jnp.where(allowed[None], scores, -1e30), axis=-1, keepdims=True)
    weights = jnp.where(allowed[None], jnp.exp(scores - top), 0.0)
    weights = (weights / jnp.sum(weights, axis=-1, keepdims=True)).astype(jnp.bfloat16)
    head_out = (
        jnp.einsum("hqk,hkc->qhc", weights, expanded[..., NOPE:], preferred_element_type=jnp.float32)
        .astype(jnp.bfloat16)
        .reshape(tok_rows, local_heads * VDIM)
    )
    attn_part = jnp.dot(head_out, o_weight, preferred_element_type=jnp.float32).astype(jnp.bfloat16)
    tp_rank = lax.axis_index("tp")
    tp_count = lax.axis_size("tp")
    share = D // tp_count
    summed = lax.dynamic_slice_in_dim(attn_part, tp_rank * share, share, 1).astype(jnp.float32)
    for d in range(1, tp_count):
        outgoing = lax.dynamic_slice_in_dim(attn_part, ((tp_rank + d) % tp_count) * share, share, 1)
        summed = summed + around(outgoing, "tp", d).astype(jnp.float32)
    hidden_cols = lax.dynamic_slice_in_dim(inputs, tp_rank * share, share, 1) + summed
    hidden_rolled = jnp.concatenate(
        [around(hidden_cols, "tp", d) for d in range(tp_count - 1, 0, -1)] + [hidden_cols], axis=1
    )
    hidden = jnp.roll(hidden_rolled, ((tp_rank + 1) % tp_count) * share, axis=1)
    mixed_in = rms_norm(hidden, ffn_gain).astype(jnp.bfloat16)
    shared_act = (
        jax.nn.silu(jnp.dot(mixed_in, shared_gate_up[0], preferred_element_type=jnp.float32))
        * jnp.dot(mixed_in, shared_gate_up[1], preferred_element_type=jnp.float32)
    ).astype(jnp.bfloat16)
    shared_part = jnp.dot(shared_act, shared_down, preferred_element_type=jnp.float32)
    experts = lax.axis_size("seq") * expert_gate_up.shape[0]
    capacity = min(tok_rows, tok_rows * TOPK * 4 // (3 * experts))
    choice_ids = expert_ids.reshape(-1)
    choice_count = choice_ids.shape[0]
    order = jnp.arange(choice_count, dtype=jnp.int32)
    earlier_same = (choice_ids[None, :] == choice_ids[:, None]) & (order[None, :] < order[:, None])
    slot_index = jnp.sum(earlier_same.astype(jnp.int32), axis=1)
    destination = choice_ids * capacity + slot_index
    source_row = order // TOPK
    out_width = mixed_in.shape[1]
    slot_source = jnp.zeros((experts * capacity,), jnp.int32).at[destination].set(source_row)
    tp_share = capacity // tp_count
    my_slots = lax.dynamic_slice_in_dim(
        slot_source.reshape(experts, capacity), tp_rank * tp_share, tp_share, 1
    )
    buffer = mixed_in[my_slots.reshape(-1)].reshape(experts, tp_share, out_width)
    hidden_part = expert_gate_up.shape[3]
    packed = jnp.concatenate(
        [expert_gate_up[0].reshape(2 * D, hidden_part), expert_down[0].T], axis=0
    )
    weight_parts = [packed] + [around(packed, "tp", d) for d in range(1, tp_count)]
    arrived = lax.all_to_all(buffer, "seq", split_axis=0, concat_axis=0, tiled=True)
    sources = arrived.shape[0]
    flat_rows = arrived.reshape(sources * tp_share, D)
    produced = None
    for part in weight_parts:
        gate_weight = part[:D]
        up_weight = part[D : 2 * D]
        down_weight_t = part[2 * D :]
        activated = (
            jax.nn.silu(jnp.dot(flat_rows, gate_weight, preferred_element_type=jnp.float32))
            * jnp.dot(flat_rows, up_weight, preferred_element_type=jnp.float32)
        ).astype(jnp.bfloat16)
        piece = lax.dot_general(
            activated, down_weight_t, (((1,), (1,)), ((), ())), preferred_element_type=jnp.float32
        ).astype(jnp.bfloat16).astype(jnp.float32)
        produced = piece if produced is None else produced + piece
    produced = produced.astype(jnp.bfloat16).reshape(sources, tp_share, D)
    returned = lax.all_to_all(produced, "seq", split_axis=0, concat_axis=0, tiled=True)
    returned = returned.reshape(experts, tp_share, tp_count, share)
    regrouped = lax.all_to_all(returned, "tp", split_axis=2, concat_axis=1, tiled=True)
    chosen = destination.reshape(tok_rows, TOPK)[:, :, None] == jnp.arange(
        experts * capacity, dtype=jnp.int32
    )[None, None, :]
    combine = jnp.sum(jnp.where(chosen, route_weight[:, :, None], 0.0), axis=1)
    routed = jnp.dot(
        combine,
        regrouped.reshape(experts * capacity, share).astype(jnp.float32),
        precision=lax.Precision.HIGHEST,
        preferred_element_type=jnp.float32,
    )
    shared_cols = lax.psum_scatter(
        shared_part.astype(jnp.bfloat16), "tp", scatter_dimension=1, tiled=True
    ).astype(jnp.float32)
    return (hidden_cols + shared_cols + routed).astype(jnp.bfloat16)


def solution(mesh):
    placed = (
        P("seq", None),
        P(),
        P(None, "tp"),
        P(),
        P(),
        P(None, "tp"),
        P("tp", None),
        P(),
        P(None, None, "tp"),
        P("tp", None),
        P("seq", None, None, "tp"),
        P("seq", "tp", None),
        P("seq", None),
        P("seq", None),
        P("seq"),
    )
    return jax.shard_map(
        local, mesh=mesh, in_specs=placed, out_specs=P("seq", "tp"), check_vma=False
    )
```

```python
import jax
import jax.numpy as jnp
from jax import lax
from jax.sharding import PartitionSpec as P

D = 2048
NOPE = 128
ROPE = 64
VDIM = 128
LATENT = 512
TOPK = 6


epsilon = 1e-06


def from_behind(block, axis, distance):
    devices = range(lax.axis_size(axis))
    route = [(i - distance, i) for i in devices if i - distance in devices]
    return lax.ppermute(block, axis, route)


def around(block, axis, distance):
    count = lax.axis_size(axis)
    return lax.ppermute(block, axis, [(i, (i + distance) % count) for i in range(count)])


def rms_norm(values, gain):
    return values * lax.rsqrt(jnp.mean(values * values, axis=-1, keepdims=True) + epsilon) * gain


def rotate(values, positions):
    half_width = values.shape[-1] // 2
    frequency = 10000.0 ** (-(jnp.arange(half_width).astype(jnp.float32) * 2.0 / values.shape[-1]))
    angles = positions[..., None] * frequency
    first_half = values[..., :half_width]
    second_half = values[..., half_width:]
    return jnp.concatenate(
        [
            first_half * jnp.cos(angles) - second_half * jnp.sin(angles),
            second_half * jnp.cos(angles) + first_half * jnp.sin(angles),
        ],
        axis=-1,
    )


def local(
    tokens,
    attn_gain,
    q_weight,
    kva_weight,
    kv_gain,
    kvb_weight,
    o_weight,
    ffn_gain,
    shared_gate_up,
    shared_down,
    expert_gate_up,
    expert_down,
    expert_ids,
    route_weight,
    segment_ids,
):
    tok_rows = tokens.shape[0]
    local_heads = q_weight.shape[1] // (NOPE + ROPE)
    first_row = lax.axis_index("seq") * tok_rows
    row_index = first_row + jnp.arange(tok_rows, dtype=jnp.int32)
    positions = row_index.astype(jnp.float32)
    inputs = tokens.astype(jnp.float32)
    normed = rms_norm(inputs, attn_gain).astype(jnp.bfloat16)
    queries = jnp.dot(normed, q_weight, preferred_element_type=jnp.float32).reshape(
        tok_rows, local_heads, NOPE + ROPE
    )
    queries = jnp.concatenate(
        [queries[..., :NOPE], rotate(queries[..., NOPE:], positions[:, None])], axis=-1
    ).astype(jnp.bfloat16)
    query_nope = queries[..., :NOPE]
    query_rope = queries[..., NOPE:]
    compressed = jnp.dot(normed, kva_weight, preferred_element_type=jnp.float32)
    latent = rms_norm(compressed[:, :LATENT], kv_gain).astype(jnp.bfloat16)
    key_rope = rotate(compressed[:, LATENT:], positions).astype(jnp.bfloat16)
    key_block = jnp.concatenate(
        [latent, key_rope, segment_ids.astype(jnp.bfloat16)[:, None]], axis=1
    )
    scale = (NOPE + ROPE) ** (-0.5)
    total_rows = lax.axis_size("seq") * tok_rows
    longest = min(4096, total_rows // 2)
    hop_count = (longest + tok_rows - 2) // tok_rows
    group = 4
    near = [from_behind(key_block, "seq", d) for d in range(group - 1, 0, -1)]
    grouped = jnp.concatenate(near + [key_block], axis=0)
    far_groups = hop_count // group
    far = [from_behind(grouped, "seq", group * m) for m in range(far_groups - 1, 0, -1)]
    singles = [from_behind(key_block, "seq", d) for d in range(hop_count, group * far_groups - 1, -1)]
    keys = jnp.concatenate(singles + far + [grouped], axis=0)
    key_count = keys.shape[0]
    key_index = first_row + tok_rows - key_count + jnp.arange(key_count, dtype=jnp.int32)
    expanded = jnp.einsum(
        "nl,lhc->hnc",
        keys[:, :LATENT],
        kvb_weight.reshape(LATENT, local_heads, NOPE + VDIM),
        preferred_element_type=jnp.float32,
    ).astype(jnp.bfloat16)
    key_full = jnp.concatenate(
        [expanded[..., :NOPE], jnp.broadcast_to(keys[None, :, LATENT : LATENT + ROPE], (local_heads, key_count, ROPE))],
        axis=-1,
    )
    scores = jnp.einsum(
        "qhc,hkc->hqk", queries, key_full, preferred_element_type=jnp.float32
    )
    scores = scores * scale
    key_ids = keys[:, LATENT + ROPE].astype(jnp.int32)
    allowed = (
        (key_ids[None, :] == segment_ids[:, None])
        & (key_index[None, :] <= row_index[:, None])
        & (key_index[None, :] >= 0)
    )
    top = jnp.max(jnp.where(allowed[None], scores, -1e30), axis=-1, keepdims=True)
    weights = jnp.where(allowed[None], jnp.exp(scores - top), 0.0)
    weights = (weights / jnp.sum(weights, axis=-1, keepdims=True)).astype(jnp.bfloat16)
    head_out = (
        jnp.einsum("hqk,hkc->qhc", weights, expanded[..., NOPE:], preferred_element_type=jnp.float32)
        .astype(jnp.bfloat16)
        .reshape(tok_rows, local_heads * VDIM)
    )
    tp_count = lax.axis_size("tp")
    hidden_part = expert_gate_up.shape[3]
    packed = jnp.concatenate(
        [expert_gate_up[0].reshape(2 * D, hidden_part), expert_down[0].T], axis=0
    )
    forward = around(packed, "tp", 1)
    backward = around(packed, "tp", tp_count - 1)
    head_out, forward, backward = lax.optimization_barrier((head_out, forward, backward))
    attn_part = jnp.dot(head_out, o_weight, preferred_element_type=jnp.float32).astype(jnp.bfloat16)
    tp_rank = lax.axis_index("tp")
    share = D // tp_count
    summed = lax.dynamic_slice_in_dim(attn_part, tp_rank * share, share, 1).astype(jnp.float32)
    for d in range(1, tp_count):
        outgoing = lax.dynamic_slice_in_dim(attn_part, ((tp_rank + d) % tp_count) * share, share, 1)
        summed = summed + around(outgoing, "tp", d).astype(jnp.float32)
    hidden_cols = lax.dynamic_slice_in_dim(inputs, tp_rank * share, share, 1) + summed
    hidden_rolled = jnp.concatenate(
        [around(hidden_cols, "tp", d) for d in range(tp_count - 1, 0, -1)] + [hidden_cols], axis=1
    )
    hidden = jnp.roll(hidden_rolled, ((tp_rank + 1) % tp_count) * share, axis=1)
    mixed_in = rms_norm(hidden, ffn_gain).astype(jnp.bfloat16)
    shared_act = (
        jax.nn.silu(jnp.dot(mixed_in, shared_gate_up[0], preferred_element_type=jnp.float32))
        * jnp.dot(mixed_in, shared_gate_up[1], preferred_element_type=jnp.float32)
    ).astype(jnp.bfloat16)
    shared_part = jnp.dot(shared_act, shared_down, preferred_element_type=jnp.float32)
    experts = lax.axis_size("seq") * expert_gate_up.shape[0]
    capacity = min(tok_rows, tok_rows * TOPK * 4 // (3 * experts))
    choice_ids = expert_ids.reshape(-1)
    choice_count = choice_ids.shape[0]
    order = jnp.arange(choice_count, dtype=jnp.int32)
    earlier_same = (choice_ids[None, :] == choice_ids[:, None]) & (order[None, :] < order[:, None])
    slot_index = jnp.sum(earlier_same.astype(jnp.int32), axis=1)
    destination = choice_ids * capacity + slot_index
    source_row = order // TOPK
    out_width = mixed_in.shape[1]
    slot_source = jnp.zeros((experts * capacity,), jnp.int32).at[destination].set(source_row)
    tp_share = capacity // tp_count
    my_slots = lax.dynamic_slice_in_dim(
        slot_source.reshape(experts, capacity), tp_rank * tp_share, tp_share, 1
    )
    buffer = mixed_in[my_slots.reshape(-1)].reshape(experts, tp_share, out_width)
    half = packed.shape[0] // 2
    far = jnp.concatenate(
        [around(forward[:half], "tp", 1), around(backward[half:], "tp", tp_count - 1)], axis=0
    )
    weight_parts = [packed, forward, backward, far]
    arrived = lax.all_to_all(buffer, "seq", split_axis=0, concat_axis=0, tiled=True)
    sources = arrived.shape[0]
    flat_rows = arrived.reshape(sources * tp_share, D)
    produced = None
    for part in weight_parts:
        gate_weight = part[:D]
        up_weight = part[D : 2 * D]
        down_weight_t = part[2 * D :]
        activated = (
            jax.nn.silu(jnp.dot(flat_rows, gate_weight, preferred_element_type=jnp.float32))
            * jnp.dot(flat_rows, up_weight, preferred_element_type=jnp.float32)
        ).astype(jnp.bfloat16)
        piece = lax.dot_general(
            activated, down_weight_t, (((1,), (1,)), ((), ())), preferred_element_type=jnp.float32
        ).astype(jnp.bfloat16).astype(jnp.float32)
        produced = piece if produced is None else produced + piece
    produced = produced.astype(jnp.bfloat16).reshape(sources, tp_share, D)
    returned = lax.all_to_all(produced, "seq", split_axis=0, concat_axis=0, tiled=True)
    returned = returned.reshape(experts, tp_share, tp_count, share)
    regrouped = lax.all_to_all(returned, "tp", split_axis=2, concat_axis=1, tiled=True)
    chosen = destination.reshape(tok_rows, TOPK)[:, :, None] == jnp.arange(
        experts * capacity, dtype=jnp.int32
    )[None, None, :]
    combine = jnp.sum(jnp.where(chosen, route_weight[:, :, None], 0.0), axis=1)
    routed = jnp.dot(
        combine,
        regrouped.reshape(experts * capacity, share).astype(jnp.float32),
        precision=lax.Precision.HIGHEST,
        preferred_element_type=jnp.float32,
    )
    shared_cols = lax.psum_scatter(
        shared_part.astype(jnp.bfloat16), "tp", scatter_dimension=1, tiled=True
    ).astype(jnp.float32)
    return (hidden_cols + shared_cols + routed).astype(jnp.bfloat16)


def solution(mesh):
    placed = (
        P("seq", None),
        P(),
        P(None, "tp"),
        P(),
        P(),
        P(None, "tp"),
        P("tp", None),
        P(),
        P(None, None, "tp"),
        P("tp", None),
        P("seq", None, None, "tp"),
        P("seq", "tp", None),
        P("seq", None),
        P("seq", None),
        P("seq"),
    )
    return jax.shard_map(
        local, mesh=mesh, in_specs=placed, out_specs=P("seq", "tp"), check_vma=False
    )
```

```python
import jax
import jax.numpy as jnp
from jax import lax
from jax.sharding import PartitionSpec as P

D = 2048
NOPE = 128
ROPE = 64
VDIM = 128
LATENT = 512
TOPK = 6


epsilon = 1e-06


def from_behind(block, axis, distance):
    devices = range(lax.axis_size(axis))
    route = [(i - distance, i) for i in devices if i - distance in devices]
    return lax.ppermute(block, axis, route)


def around(block, axis, distance):
    count = lax.axis_size(axis)
    return lax.ppermute(block, axis, [(i, (i + distance) % count) for i in range(count)])


def rms_norm(values, gain):
    return values * lax.rsqrt(jnp.mean(values * values, axis=-1, keepdims=True) + epsilon) * gain


def rotate(values, positions):
    half_width = values.shape[-1] // 2
    frequency = 10000.0 ** (-(jnp.arange(half_width).astype(jnp.float32) * 2.0 / values.shape[-1]))
    angles = positions[..., None] * frequency
    first_half = values[..., :half_width]
    second_half = values[..., half_width:]
    return jnp.concatenate(
        [
            first_half * jnp.cos(angles) - second_half * jnp.sin(angles),
            second_half * jnp.cos(angles) + first_half * jnp.sin(angles),
        ],
        axis=-1,
    )


def local(
    tokens,
    attn_gain,
    q_weight,
    kva_weight,
    kv_gain,
    kvb_weight,
    o_weight,
    ffn_gain,
    shared_gate_up,
    shared_down,
    expert_gate_up,
    expert_down,
    expert_ids,
    route_weight,
    segment_ids,
):
    tok_rows = tokens.shape[0]
    local_heads = q_weight.shape[1] // (NOPE + ROPE)
    first_row = lax.axis_index("seq") * tok_rows
    row_index = first_row + jnp.arange(tok_rows, dtype=jnp.int32)
    positions = row_index.astype(jnp.float32)
    inputs = tokens.astype(jnp.float32)
    normed = rms_norm(inputs, attn_gain).astype(jnp.bfloat16)
    queries = jnp.dot(normed, q_weight, preferred_element_type=jnp.float32).reshape(
        tok_rows, local_heads, NOPE + ROPE
    )
    queries = jnp.concatenate(
        [queries[..., :NOPE], rotate(queries[..., NOPE:], positions[:, None])], axis=-1
    ).astype(jnp.bfloat16)
    query_nope = queries[..., :NOPE]
    query_rope = queries[..., NOPE:]
    compressed = jnp.dot(normed, kva_weight, preferred_element_type=jnp.float32)
    latent = rms_norm(compressed[:, :LATENT], kv_gain).astype(jnp.bfloat16)
    key_rope = rotate(compressed[:, LATENT:], positions).astype(jnp.bfloat16)
    key_block = jnp.concatenate(
        [latent, key_rope, segment_ids.astype(jnp.bfloat16)[:, None]], axis=1
    )
    scale = (NOPE + ROPE) ** (-0.5)
    total_rows = lax.axis_size("seq") * tok_rows
    longest = min(4096, total_rows // 2)
    hop_count = (longest + tok_rows - 2) // tok_rows
    group = 4
    near = [from_behind(key_block, "seq", d) for d in range(group - 1, 0, -1)]
    grouped = jnp.concatenate(near + [key_block], axis=0)
    far_groups = hop_count // group
    far = [from_behind(grouped, "seq", group * m) for m in range(far_groups - 1, 0, -1)]
    singles = [from_behind(key_block, "seq", d) for d in range(hop_count, group * far_groups - 1, -1)]
    keys = jnp.concatenate(singles + far + [grouped], axis=0)
    key_count = keys.shape[0]
    key_index = first_row + tok_rows - key_count + jnp.arange(key_count, dtype=jnp.int32)
    expanded = jnp.einsum(
        "nl,lhc->hnc",
        keys[:, :LATENT],
        kvb_weight.reshape(LATENT, local_heads, NOPE + VDIM),
        preferred_element_type=jnp.float32,
    ).astype(jnp.bfloat16)
    key_full = jnp.concatenate(
        [expanded[..., :NOPE], jnp.broadcast_to(keys[None, :, LATENT : LATENT + ROPE], (local_heads, key_count, ROPE))],
        axis=-1,
    )
    scores = jnp.einsum(
        "qhc,hkc->hqk", queries, key_full, preferred_element_type=jnp.float32
    )
    scores = scores * scale
    key_ids = keys[:, LATENT + ROPE].astype(jnp.int32)
    allowed = (
        (key_ids[None, :] == segment_ids[:, None])
        & (key_index[None, :] <= row_index[:, None])
        & (key_index[None, :] >= 0)
    )
    top = jnp.max(jnp.where(allowed[None], scores, -1e30), axis=-1, keepdims=True)
    weights = jnp.where(allowed[None], jnp.exp(scores - top), 0.0)
    denominator = jnp.sum(weights, axis=-1)
    mixed = jnp.einsum(
        "hqk,hkc->hqc", weights.astype(jnp.bfloat16), expanded[..., NOPE:], preferred_element_type=jnp.float32
    )
    head_out = (
        (mixed / denominator[..., None])
        .astype(jnp.bfloat16)
        .transpose(1, 0, 2)
        .reshape(tok_rows, local_heads * VDIM)
    )
    tp_count = lax.axis_size("tp")
    hidden_part = expert_gate_up.shape[3]
    packed = jnp.concatenate(
        [expert_gate_up[0].reshape(2 * D, hidden_part), expert_down[0].reshape(D, hidden_part)], axis=0
    )
    forward = around(packed, "tp", 1)
    backward = around(packed, "tp", tp_count - 1)
    head_out, forward, backward = lax.optimization_barrier((head_out, forward, backward))
    attn_part = jnp.dot(head_out, o_weight, preferred_element_type=jnp.float32).astype(jnp.bfloat16)
    tp_rank = lax.axis_index("tp")
    share = D // tp_count
    summed = lax.dynamic_slice_in_dim(attn_part, tp_rank * share, share, 1).astype(jnp.float32)
    for d in range(1, tp_count):
        outgoing = lax.dynamic_slice_in_dim(attn_part, ((tp_rank + d) % tp_count) * share, share, 1)
        summed = summed + around(outgoing, "tp", d).astype(jnp.float32)
    hidden_cols = lax.dynamic_slice_in_dim(inputs, tp_rank * share, share, 1) + summed
    hidden_rolled = jnp.concatenate(
        [around(hidden_cols, "tp", d) for d in range(tp_count - 1, 0, -1)] + [hidden_cols], axis=1
    )
    hidden = jnp.roll(hidden_rolled, ((tp_rank + 1) % tp_count) * share, axis=1)
    mixed_in = rms_norm(hidden, ffn_gain).astype(jnp.bfloat16)
    shared_act = (
        jax.nn.silu(jnp.dot(mixed_in, shared_gate_up[0], preferred_element_type=jnp.float32))
        * jnp.dot(mixed_in, shared_gate_up[1], preferred_element_type=jnp.float32)
    ).astype(jnp.bfloat16)
    shared_part = jnp.dot(shared_act, shared_down, preferred_element_type=jnp.float32)
    experts = lax.axis_size("seq") * expert_gate_up.shape[0]
    capacity = min(tok_rows, tok_rows * TOPK * 4 // (3 * experts))
    choice_ids = expert_ids.reshape(-1)
    choice_count = choice_ids.shape[0]
    order = jnp.arange(choice_count, dtype=jnp.int32)
    earlier_same = (choice_ids[None, :] == choice_ids[:, None]) & (order[None, :] < order[:, None])
    slot_index = jnp.sum(earlier_same.astype(jnp.int32), axis=1)
    destination = choice_ids * capacity + slot_index
    source_row = order // TOPK
    out_width = mixed_in.shape[1]
    slot_source = jnp.zeros((experts * capacity,), jnp.int32).at[destination].set(source_row)
    tp_share = capacity // tp_count
    my_slots = lax.dynamic_slice_in_dim(
        slot_source.reshape(experts, capacity), tp_rank * tp_share, tp_share, 1
    )
    buffer = mixed_in[my_slots.reshape(-1)].reshape(experts, tp_share, out_width)
    half = packed.shape[0] // 2
    far = jnp.concatenate(
        [around(forward[:half], "tp", 1), around(backward[half:], "tp", tp_count - 1)], axis=0
    )
    weight_parts = [packed, forward, backward, far]
    arrived = lax.all_to_all(buffer, "seq", split_axis=0, concat_axis=0, tiled=True)
    sources = arrived.shape[0]
    flat_rows = arrived.reshape(sources * tp_share, D)
    produced = None
    for part in weight_parts:
        gate_weight = part[:D]
        up_weight = part[D : 2 * D]
        down_weight = part[2 * D :].reshape(hidden_part, D)
        activated = (
            jax.nn.silu(jnp.dot(flat_rows, gate_weight, preferred_element_type=jnp.float32))
            * jnp.dot(flat_rows, up_weight, preferred_element_type=jnp.float32)
        ).astype(jnp.bfloat16)
        piece = jnp.dot(activated, down_weight, preferred_element_type=jnp.float32).astype(
            jnp.bfloat16
        ).astype(jnp.float32)
        produced = piece if produced is None else produced + piece
    produced = produced.astype(jnp.bfloat16).reshape(sources, tp_share, D)
    returned = lax.all_to_all(produced, "seq", split_axis=0, concat_axis=0, tiled=True)
    returned = returned.reshape(experts, tp_share, tp_count, share)
    regrouped = lax.all_to_all(returned, "tp", split_axis=2, concat_axis=1, tiled=True)
    chosen = destination.reshape(tok_rows, TOPK)[:, :, None] == jnp.arange(
        experts * capacity, dtype=jnp.int32
    )[None, None, :]
    combine = jnp.sum(jnp.where(chosen, route_weight[:, :, None], 0.0), axis=1)
    routed = jnp.dot(
        combine,
        regrouped.reshape(experts * capacity, share).astype(jnp.float32),
        precision=lax.Precision.HIGHEST,
        preferred_element_type=jnp.float32,
    )
    shared_cols = lax.psum_scatter(
        shared_part.astype(jnp.bfloat16), "tp", scatter_dimension=1, tiled=True
    ).astype(jnp.float32)
    return (hidden_cols + shared_cols + routed).astype(jnp.bfloat16)


def solution(mesh):
    placed = (
        P("seq", None),
        P(),
        P(None, "tp"),
        P(),
        P(),
        P(None, "tp"),
        P("tp", None),
        P(),
        P(None, None, "tp"),
        P("tp", None),
        P("seq", None, None, "tp"),
        P("seq", "tp", None),
        P("seq", None),
        P("seq", None),
        P("seq"),
    )
    return jax.shard_map(
        local, mesh=mesh, in_specs=placed, out_specs=P("seq", "tp"), check_vma=False
    )
```

```python
import jax
import jax.numpy as jnp
from jax import lax
from jax.sharding import PartitionSpec as P

D = 2048
NOPE = 128
ROPE = 64
VDIM = 128
LATENT = 512
TOPK = 6


epsilon = 1e-06


def from_behind(block, axis, distance):
    devices = range(lax.axis_size(axis))
    route = [(i - distance, i) for i in devices if i - distance in devices]
    return lax.ppermute(block, axis, route)


def around(block, axis, distance):
    count = lax.axis_size(axis)
    return lax.ppermute(block, axis, [(i, (i + distance) % count) for i in range(count)])


def rms_norm(values, gain):
    return values * lax.rsqrt(jnp.mean(values * values, axis=-1, keepdims=True) + epsilon) * gain


def rotate(values, positions):
    half_width = values.shape[-1] // 2
    frequency = 10000.0 ** (-(jnp.arange(half_width).astype(jnp.float32) * 2.0 / values.shape[-1]))
    angles = positions[..., None] * frequency
    first_half = values[..., :half_width]
    second_half = values[..., half_width:]
    return jnp.concatenate(
        [
            first_half * jnp.cos(angles) - second_half * jnp.sin(angles),
            second_half * jnp.cos(angles) + first_half * jnp.sin(angles),
        ],
        axis=-1,
    )


def local(
    tokens,
    attn_gain,
    q_weight,
    kva_weight,
    kv_gain,
    kvb_weight,
    o_weight,
    ffn_gain,
    shared_gate_up,
    shared_down,
    expert_gate_up,
    expert_down,
    expert_ids,
    route_weight,
    segment_ids,
):
    tok_rows = tokens.shape[0]
    local_heads = q_weight.shape[1] // (NOPE + ROPE)
    first_row = lax.axis_index("seq") * tok_rows
    row_index = first_row + jnp.arange(tok_rows, dtype=jnp.int32)
    positions = row_index.astype(jnp.float32)
    inputs = tokens.astype(jnp.float32)
    normed = rms_norm(inputs, attn_gain).astype(jnp.bfloat16)
    queries = jnp.dot(normed, q_weight, preferred_element_type=jnp.float32).reshape(
        tok_rows, local_heads, NOPE + ROPE
    )
    queries = jnp.concatenate(
        [queries[..., :NOPE], rotate(queries[..., NOPE:], positions[:, None])], axis=-1
    ).astype(jnp.bfloat16)
    query_nope = queries[..., :NOPE]
    query_rope = queries[..., NOPE:]
    compressed = jnp.dot(normed, kva_weight, preferred_element_type=jnp.float32)
    latent = rms_norm(compressed[:, :LATENT], kv_gain).astype(jnp.bfloat16)
    key_rope = rotate(compressed[:, LATENT:], positions).astype(jnp.bfloat16)
    key_block = jnp.concatenate(
        [latent, key_rope, segment_ids.astype(jnp.bfloat16)[:, None]], axis=1
    )
    scale = (NOPE + ROPE) ** (-0.5)
    total_rows = lax.axis_size("seq") * tok_rows
    longest = min(4096, total_rows // 2)
    hop_count = (longest + tok_rows - 2) // tok_rows
    group = 4
    near = [from_behind(key_block, "seq", d) for d in range(group - 1, 0, -1)]
    grouped = jnp.concatenate(near + [key_block], axis=0)
    far_groups = hop_count // group
    far = [from_behind(grouped, "seq", group * m) for m in range(far_groups - 1, 0, -1)]
    singles = [from_behind(key_block, "seq", d) for d in range(hop_count, group * far_groups - 1, -1)]
    keys = jnp.concatenate(singles + far + [grouped], axis=0)
    key_count = keys.shape[0]
    key_index = first_row + tok_rows - key_count + jnp.arange(key_count, dtype=jnp.int32)
    expanded = jnp.einsum(
        "nl,lhc->hnc",
        keys[:, :LATENT],
        kvb_weight.reshape(LATENT, local_heads, NOPE + VDIM),
        preferred_element_type=jnp.float32,
    ).astype(jnp.bfloat16)
    key_full = jnp.concatenate(
        [expanded[..., :NOPE], jnp.broadcast_to(keys[None, :, LATENT : LATENT + ROPE], (local_heads, key_count, ROPE))],
        axis=-1,
    )
    scores = jnp.einsum(
        "qhc,hkc->hqk", queries, key_full, preferred_element_type=jnp.float32
    )
    scores = scores * scale
    key_ids = keys[:, LATENT + ROPE].astype(jnp.int32)
    allowed = (
        (key_ids[None, :] == segment_ids[:, None])
        & (key_index[None, :] <= row_index[:, None])
        & (key_index[None, :] >= 0)
    )
    top = jnp.max(jnp.where(allowed[None], scores, -1e30), axis=-1, keepdims=True)
    weights = jnp.where(allowed[None], jnp.exp(scores - top), 0.0)
    denominator = jnp.sum(weights, axis=-1)
    mixed = jnp.einsum(
        "hqk,hkc->hqc", weights.astype(jnp.bfloat16), expanded[..., NOPE:], preferred_element_type=jnp.float32
    )
    head_out = (
        (mixed / denominator[..., None])
        .astype(jnp.bfloat16)
        .transpose(1, 0, 2)
        .reshape(tok_rows, local_heads * VDIM)
    )
    tp_count = lax.axis_size("tp")
    hidden_part = expert_gate_up.shape[3]
    packed = jnp.concatenate(
        [expert_gate_up[0].reshape(2 * D, hidden_part), expert_down[0].T], axis=0
    )
    forward = around(packed, "tp", 1)
    backward = around(packed, "tp", tp_count - 1)
    head_out, forward, backward = lax.optimization_barrier((head_out, forward, backward))
    attn_part = jnp.dot(head_out, o_weight, preferred_element_type=jnp.float32).astype(jnp.bfloat16)
    tp_rank = lax.axis_index("tp")
    share = D // tp_count
    summed = lax.dynamic_slice_in_dim(attn_part, tp_rank * share, share, 1).astype(jnp.float32)
    for d in range(1, tp_count):
        outgoing = lax.dynamic_slice_in_dim(attn_part, ((tp_rank + d) % tp_count) * share, share, 1)
        summed = summed + around(outgoing, "tp", d).astype(jnp.float32)
    hidden_cols = lax.dynamic_slice_in_dim(inputs, tp_rank * share, share, 1) + summed
    hidden_rolled = jnp.concatenate(
        [around(hidden_cols, "tp", d) for d in range(tp_count - 1, 0, -1)] + [hidden_cols], axis=1
    )
    hidden = jnp.roll(hidden_rolled, ((tp_rank + 1) % tp_count) * share, axis=1)
    mixed_in = rms_norm(hidden, ffn_gain).astype(jnp.bfloat16)
    shared_act = (
        jax.nn.silu(jnp.dot(mixed_in, shared_gate_up[0], preferred_element_type=jnp.float32))
        * jnp.dot(mixed_in, shared_gate_up[1], preferred_element_type=jnp.float32)
    ).astype(jnp.bfloat16)
    shared_part = jnp.dot(shared_act, shared_down, preferred_element_type=jnp.float32)
    experts = lax.axis_size("seq") * expert_gate_up.shape[0]
    capacity = min(tok_rows, tok_rows * TOPK * 4 // (3 * experts))
    choice_ids = expert_ids.reshape(-1)
    choice_count = choice_ids.shape[0]
    order = jnp.arange(choice_count, dtype=jnp.int32)
    earlier_same = (choice_ids[None, :] == choice_ids[:, None]) & (order[None, :] < order[:, None])
    slot_index = jnp.sum(earlier_same.astype(jnp.int32), axis=1)
    destination = choice_ids * capacity + slot_index
    source_row = order // TOPK
    out_width = mixed_in.shape[1]
    slot_source = jnp.zeros((experts * capacity,), jnp.int32).at[destination].set(source_row)
    tp_share = capacity // tp_count
    my_slots = lax.dynamic_slice_in_dim(
        slot_source.reshape(experts, capacity), tp_rank * tp_share, tp_share, 1
    )
    buffer = mixed_in[my_slots.reshape(-1)].reshape(experts, tp_share, out_width)
    half = packed.shape[0] // 2
    far = jnp.concatenate(
        [around(forward[:half], "tp", 1), around(backward[half:], "tp", tp_count - 1)], axis=0
    )
    weight_parts = [packed, forward, backward, far]
    arrived = lax.all_to_all(buffer, "seq", split_axis=0, concat_axis=0, tiled=True)
    sources = arrived.shape[0]
    flat_rows = arrived.reshape(sources * tp_share, D)
    produced = None
    for part in weight_parts:
        gate_weight = part[:D]
        up_weight = part[D : 2 * D]
        down_weight_t = part[2 * D :]
        activated = (
            jax.nn.silu(jnp.dot(flat_rows, gate_weight, preferred_element_type=jnp.float32))
            * jnp.dot(flat_rows, up_weight, preferred_element_type=jnp.float32)
        ).astype(jnp.bfloat16)
        piece = lax.dot_general(
            activated, down_weight_t, (((1,), (1,)), ((), ())), preferred_element_type=jnp.float32
        ).astype(jnp.bfloat16).astype(jnp.float32)
        produced = piece if produced is None else produced + piece
    produced = produced.astype(jnp.bfloat16).reshape(sources, tp_share, D)
    returned = lax.all_to_all(produced, "seq", split_axis=0, concat_axis=0, tiled=True)
    returned = returned.reshape(experts * tp_share, D).astype(jnp.float32)
    choice_slot = slot_index.reshape(tok_rows, TOPK)
    local_row = choice_ids.reshape(tok_rows, TOPK) * tp_share + choice_slot % tp_share
    mine = (choice_slot // tp_share) == tp_rank
    chosen = local_row[:, :, None] == jnp.arange(experts * tp_share, dtype=jnp.int32)[None, None, :]
    combine = jnp.sum(jnp.where(chosen & mine[:, :, None], route_weight[:, :, None], 0.0), axis=1)
    routed_part = jnp.dot(
        combine, returned, precision=lax.Precision.HIGHEST, preferred_element_type=jnp.float32
    )
    routed = lax.dynamic_slice_in_dim(routed_part, tp_rank * share, share, 1)
    for d in range(1, tp_count):
        outgoing = lax.dynamic_slice_in_dim(routed_part, ((tp_rank + d) % tp_count) * share, share, 1)
        routed = routed + around(outgoing, "tp", d)
    shared_cols = lax.psum_scatter(
        shared_part.astype(jnp.bfloat16), "tp", scatter_dimension=1, tiled=True
    ).astype(jnp.float32)
    return (hidden_cols + shared_cols + routed).astype(jnp.bfloat16)


def solution(mesh):
    placed = (
        P("seq", None),
        P(),
        P(None, "tp"),
        P(),
        P(),
        P(None, "tp"),
        P("tp", None),
        P(),
        P(None, None, "tp"),
        P("tp", None),
        P("seq", None, None, "tp"),
        P("seq", "tp", None),
        P("seq", None),
        P("seq", None),
        P("seq"),
    )
    return jax.shard_map(
        local, mesh=mesh, in_specs=placed, out_specs=P("seq", "tp"), check_vma=False
    )
```

```python
import jax
import jax.numpy as jnp
from jax import lax
from jax.sharding import PartitionSpec as P

D = 2048
NOPE = 128
ROPE = 64
VDIM = 128
LATENT = 512
TOPK = 6


epsilon = 1e-06


def from_behind(block, axis, distance):
    devices = range(lax.axis_size(axis))
    route = [(i - distance, i) for i in devices if i - distance in devices]
    return lax.ppermute(block, axis, route)


def around(block, axis, distance):
    count = lax.axis_size(axis)
    return lax.ppermute(block, axis, [(i, (i + distance) % count) for i in range(count)])


def rms_norm(values, gain):
    return values * lax.rsqrt(jnp.mean(values * values, axis=-1, keepdims=True) + epsilon) * gain


def rotate(values, positions):
    half_width = values.shape[-1] // 2
    frequency = 10000.0 ** (-(jnp.arange(half_width).astype(jnp.float32) * 2.0 / values.shape[-1]))
    angles = positions[..., None] * frequency
    first_half = values[..., :half_width]
    second_half = values[..., half_width:]
    return jnp.concatenate(
        [
            first_half * jnp.cos(angles) - second_half * jnp.sin(angles),
            second_half * jnp.cos(angles) + first_half * jnp.sin(angles),
        ],
        axis=-1,
    )


def local(
    tokens,
    attn_gain,
    q_weight,
    kva_weight,
    kv_gain,
    kvb_weight,
    o_weight,
    ffn_gain,
    shared_gate_up,
    shared_down,
    expert_gate_up,
    expert_down,
    expert_ids,
    route_weight,
    segment_ids,
):
    tok_rows = tokens.shape[0]
    local_heads = q_weight.shape[1] // (NOPE + ROPE)
    first_row = lax.axis_index("seq") * tok_rows
    row_index = first_row + jnp.arange(tok_rows, dtype=jnp.int32)
    positions = row_index.astype(jnp.float32)
    inputs = tokens.astype(jnp.float32)
    normed = rms_norm(inputs, attn_gain).astype(jnp.bfloat16)
    queries = jnp.dot(normed, q_weight, preferred_element_type=jnp.float32).reshape(
        tok_rows, local_heads, NOPE + ROPE
    )
    queries = jnp.concatenate(
        [queries[..., :NOPE], rotate(queries[..., NOPE:], positions[:, None])], axis=-1
    ).astype(jnp.bfloat16)
    query_nope = queries[..., :NOPE]
    query_rope = queries[..., NOPE:]
    compressed = jnp.dot(normed, kva_weight, preferred_element_type=jnp.float32)
    latent = rms_norm(compressed[:, :LATENT], kv_gain).astype(jnp.bfloat16)
    key_rope = rotate(compressed[:, LATENT:], positions).astype(jnp.bfloat16)
    key_block = jnp.concatenate(
        [latent, key_rope, segment_ids.astype(jnp.bfloat16)[:, None]], axis=1
    )
    scale = (NOPE + ROPE) ** (-0.5)
    total_rows = lax.axis_size("seq") * tok_rows
    longest = min(4096, total_rows // 2)
    hop_count = (longest + tok_rows - 2) // tok_rows
    group = 4
    near = [from_behind(key_block, "seq", d) for d in range(group - 1, 0, -1)]
    grouped = jnp.concatenate(near + [key_block], axis=0)
    far_groups = hop_count // group
    far = [from_behind(grouped, "seq", group * m) for m in range(far_groups - 1, 0, -1)]
    singles = [from_behind(key_block, "seq", d) for d in range(hop_count, group * far_groups - 1, -1)]
    expand = kvb_weight.reshape(LATENT, local_heads, NOPE + VDIM)

    def attend_part(keys, first_key):
        count = keys.shape[0]
        key_index = first_key + jnp.arange(count, dtype=jnp.int32)
        expanded = jnp.einsum(
            "nl,lhc->hnc", keys[:, :LATENT], expand, preferred_element_type=jnp.float32
        ).astype(jnp.bfloat16)
        key_full = jnp.concatenate(
            [
                expanded[..., :NOPE],
                jnp.broadcast_to(keys[None, :, LATENT : LATENT + ROPE], (local_heads, count, ROPE)),
            ],
            axis=-1,
        )
        scores = jnp.einsum("qhc,hkc->hqk", queries, key_full, preferred_element_type=jnp.float32)
        scores = scores * scale
        key_ids = keys[:, LATENT + ROPE].astype(jnp.int32)
        allowed = (
            (key_ids[None, :] == segment_ids[:, None])
            & (key_index[None, :] <= row_index[:, None])
            & (key_index[None, :] >= 0)
        )
        top = jnp.max(jnp.where(allowed[None], scores, -1e30), axis=-1)
        weights = jnp.where(allowed[None], jnp.exp(scores - top[..., None]), 0.0)
        mixed = jnp.einsum(
            "hqk,hkc->hqc", weights.astype(jnp.bfloat16), expanded[..., NOPE:],
            preferred_element_type=jnp.float32,
        )
        return top, jnp.sum(weights, axis=-1), mixed

    near_top, near_sum, near_out = attend_part(grouped, first_row - (group - 1) * tok_rows)
    far_keys = jnp.concatenate(singles + far, axis=0)
    far_top, far_sum, far_out = attend_part(far_keys, first_row - hop_count * tok_rows)
    top = jnp.maximum(near_top, far_top)
    near_scale = jnp.exp(near_top - top)
    far_scale = jnp.exp(far_top - top)
    denominator = near_sum * near_scale + far_sum * far_scale
    mixed = near_out * near_scale[..., None] + far_out * far_scale[..., None]
    head_out = (
        (mixed / denominator[..., None])
        .astype(jnp.bfloat16)
        .transpose(1, 0, 2)
        .reshape(tok_rows, local_heads * VDIM)
    )
    tp_count = lax.axis_size("tp")
    hidden_part = expert_gate_up.shape[3]
    packed = jnp.concatenate(
        [expert_gate_up[0].reshape(2 * D, hidden_part), expert_down[0].T], axis=0
    )
    forward = around(packed, "tp", 1)
    backward = around(packed, "tp", tp_count - 1)
    head_out, forward, backward = lax.optimization_barrier((head_out, forward, backward))
    attn_part = jnp.dot(head_out, o_weight, preferred_element_type=jnp.float32).astype(jnp.bfloat16)
    tp_rank = lax.axis_index("tp")
    share = D // tp_count
    summed = lax.dynamic_slice_in_dim(attn_part, tp_rank * share, share, 1).astype(jnp.float32)
    for d in range(1, tp_count):
        outgoing = lax.dynamic_slice_in_dim(attn_part, ((tp_rank + d) % tp_count) * share, share, 1)
        summed = summed + around(outgoing, "tp", d).astype(jnp.float32)
    hidden_cols = lax.dynamic_slice_in_dim(inputs, tp_rank * share, share, 1) + summed
    hidden_rolled = jnp.concatenate(
        [around(hidden_cols, "tp", d) for d in range(tp_count - 1, 0, -1)] + [hidden_cols], axis=1
    )
    hidden = jnp.roll(hidden_rolled, ((tp_rank + 1) % tp_count) * share, axis=1)
    mixed_in = rms_norm(hidden, ffn_gain).astype(jnp.bfloat16)
    shared_act = (
        jax.nn.silu(jnp.dot(mixed_in, shared_gate_up[0], preferred_element_type=jnp.float32))
        * jnp.dot(mixed_in, shared_gate_up[1], preferred_element_type=jnp.float32)
    ).astype(jnp.bfloat16)
    shared_part = jnp.dot(shared_act, shared_down, preferred_element_type=jnp.float32)
    experts = lax.axis_size("seq") * expert_gate_up.shape[0]
    capacity = min(tok_rows, tok_rows * TOPK * 4 // (3 * experts))
    choice_ids = expert_ids.reshape(-1)
    choice_count = choice_ids.shape[0]
    order = jnp.arange(choice_count, dtype=jnp.int32)
    earlier_same = (choice_ids[None, :] == choice_ids[:, None]) & (order[None, :] < order[:, None])
    slot_index = jnp.sum(earlier_same.astype(jnp.int32), axis=1)
    destination = choice_ids * capacity + slot_index
    source_row = order // TOPK
    out_width = mixed_in.shape[1]
    slot_source = jnp.zeros((experts * capacity,), jnp.int32).at[destination].set(source_row)
    tp_share = capacity // tp_count
    my_slots = lax.dynamic_slice_in_dim(
        slot_source.reshape(experts, capacity), tp_rank * tp_share, tp_share, 1
    )
    buffer = mixed_in[my_slots.reshape(-1)].reshape(experts, tp_share, out_width)
    half = packed.shape[0] // 2
    far = jnp.concatenate(
        [around(forward[:half], "tp", 1), around(backward[half:], "tp", tp_count - 1)], axis=0
    )
    weight_parts = [packed, forward, backward, far]
    arrived = lax.all_to_all(buffer, "seq", split_axis=0, concat_axis=0, tiled=True)
    sources = arrived.shape[0]
    flat_rows = arrived.reshape(sources * tp_share, D)
    produced = None
    for part in weight_parts:
        gate_weight = part[:D]
        up_weight = part[D : 2 * D]
        down_weight_t = part[2 * D :]
        activated = (
            jax.nn.silu(jnp.dot(flat_rows, gate_weight, preferred_element_type=jnp.float32))
            * jnp.dot(flat_rows, up_weight, preferred_element_type=jnp.float32)
        ).astype(jnp.bfloat16)
        piece = lax.dot_general(
            activated, down_weight_t, (((1,), (1,)), ((), ())), preferred_element_type=jnp.float32
        ).astype(jnp.bfloat16).astype(jnp.float32)
        produced = piece if produced is None else produced + piece
    produced = produced.astype(jnp.bfloat16).reshape(sources, tp_share, D)
    returned = lax.all_to_all(produced, "seq", split_axis=0, concat_axis=0, tiled=True)
    returned = returned.reshape(experts * tp_share, D).astype(jnp.float32)
    choice_slot = slot_index.reshape(tok_rows, TOPK)
    local_row = choice_ids.reshape(tok_rows, TOPK) * tp_share + choice_slot % tp_share
    mine = (choice_slot // tp_share) == tp_rank
    chosen = local_row[:, :, None] == jnp.arange(experts * tp_share, dtype=jnp.int32)[None, None, :]
    combine = jnp.sum(jnp.where(chosen & mine[:, :, None], route_weight[:, :, None], 0.0), axis=1)
    routed_part = jnp.dot(
        combine, returned, precision=lax.Precision.HIGHEST, preferred_element_type=jnp.float32
    )
    routed = lax.dynamic_slice_in_dim(routed_part, tp_rank * share, share, 1)
    for d in range(1, tp_count):
        outgoing = lax.dynamic_slice_in_dim(routed_part, ((tp_rank + d) % tp_count) * share, share, 1)
        routed = routed + around(outgoing, "tp", d)
    shared_cols = lax.psum_scatter(
        shared_part.astype(jnp.bfloat16), "tp", scatter_dimension=1, tiled=True
    ).astype(jnp.float32)
    return (hidden_cols + shared_cols + routed).astype(jnp.bfloat16)


def solution(mesh):
    placed = (
        P("seq", None),
        P(),
        P(None, "tp"),
        P(),
        P(),
        P(None, "tp"),
        P("tp", None),
        P(),
        P(None, None, "tp"),
        P("tp", None),
        P("seq", None, None, "tp"),
        P("seq", "tp", None),
        P("seq", None),
        P("seq", None),
        P("seq"),
    )
    return jax.shard_map(
        local, mesh=mesh, in_specs=placed, out_specs=P("seq", "tp"), check_vma=False
    )
```

```python
import jax
import jax.numpy as jnp
from jax import lax
from jax.sharding import PartitionSpec as P

D = 2048
NOPE = 128
ROPE = 64
VDIM = 128
LATENT = 512
TOPK = 6


epsilon = 1e-06


def from_behind(block, axis, distance):
    devices = range(lax.axis_size(axis))
    route = [(i - distance, i) for i in devices if i - distance in devices]
    return lax.ppermute(block, axis, route)


def around(block, axis, distance):
    count = lax.axis_size(axis)
    return lax.ppermute(block, axis, [(i, (i + distance) % count) for i in range(count)])


def rms_norm(values, gain):
    return values * lax.rsqrt(jnp.mean(values * values, axis=-1, keepdims=True) + epsilon) * gain


def rotate(values, positions):
    half_width = values.shape[-1] // 2
    frequency = 10000.0 ** (-(jnp.arange(half_width).astype(jnp.float32) * 2.0 / values.shape[-1]))
    angles = positions[..., None] * frequency
    first_half = values[..., :half_width]
    second_half = values[..., half_width:]
    return jnp.concatenate(
        [
            first_half * jnp.cos(angles) - second_half * jnp.sin(angles),
            second_half * jnp.cos(angles) + first_half * jnp.sin(angles),
        ],
        axis=-1,
    )


def local(
    tokens,
    attn_gain,
    q_weight,
    kva_weight,
    kv_gain,
    kvb_weight,
    o_weight,
    ffn_gain,
    shared_gate_up,
    shared_down,
    expert_gate_up,
    expert_down,
    expert_ids,
    route_weight,
    segment_ids,
):
    tok_rows = tokens.shape[0]
    local_heads = q_weight.shape[1] // (NOPE + ROPE)
    first_row = lax.axis_index("seq") * tok_rows
    row_index = first_row + jnp.arange(tok_rows, dtype=jnp.int32)
    positions = row_index.astype(jnp.float32)
    inputs = tokens.astype(jnp.float32)
    normed = rms_norm(inputs, attn_gain).astype(jnp.bfloat16)
    queries = jnp.dot(normed, q_weight, preferred_element_type=jnp.float32).reshape(
        tok_rows, local_heads, NOPE + ROPE
    )
    queries = jnp.concatenate(
        [queries[..., :NOPE], rotate(queries[..., NOPE:], positions[:, None])], axis=-1
    ).astype(jnp.bfloat16)
    query_nope = queries[..., :NOPE]
    query_rope = queries[..., NOPE:]
    compressed = jnp.dot(normed, kva_weight, preferred_element_type=jnp.float32)
    latent = rms_norm(compressed[:, :LATENT], kv_gain).astype(jnp.bfloat16)
    key_rope = rotate(compressed[:, LATENT:], positions).astype(jnp.bfloat16)
    key_block = jnp.concatenate(
        [latent, key_rope, segment_ids.astype(jnp.bfloat16)[:, None]], axis=1
    )
    scale = (NOPE + ROPE) ** (-0.5)
    total_rows = lax.axis_size("seq") * tok_rows
    longest = min(4096, total_rows // 2)
    hop_count = (longest + tok_rows - 2) // tok_rows
    group = 4
    near = [from_behind(key_block, "seq", d) for d in range(group - 1, 0, -1)]
    grouped = jnp.concatenate(near + [key_block], axis=0)
    far_groups = hop_count // group
    far = [from_behind(grouped, "seq", group * m) for m in range(far_groups - 1, 0, -1)]
    singles = [from_behind(key_block, "seq", d) for d in range(hop_count, group * far_groups - 1, -1)]
    keys = jnp.concatenate(singles + far + [grouped], axis=0)
    key_count = keys.shape[0]
    key_index = first_row + tok_rows - key_count + jnp.arange(key_count, dtype=jnp.int32)
    expanded = jnp.einsum(
        "nl,lhc->hnc",
        keys[:, :LATENT],
        kvb_weight.reshape(LATENT, local_heads, NOPE + VDIM),
        preferred_element_type=jnp.float32,
    ).astype(jnp.bfloat16)
    key_full = jnp.concatenate(
        [expanded[..., :NOPE], jnp.broadcast_to(keys[None, :, LATENT : LATENT + ROPE], (local_heads, key_count, ROPE))],
        axis=-1,
    )
    scores = jnp.einsum(
        "qhc,hkc->hqk", queries, key_full, preferred_element_type=jnp.float32
    )
    scores = scores * scale
    key_ids = keys[:, LATENT + ROPE].astype(jnp.int32)
    allowed = (
        (key_ids[None, :] == segment_ids[:, None])
        & (key_index[None, :] <= row_index[:, None])
        & (key_index[None, :] >= 0)
    )
    top = jnp.max(jnp.where(allowed[None], scores, -1e30), axis=-1, keepdims=True)
    weights = jnp.where(allowed[None], jnp.exp(scores - top), 0.0)
    denominator = jnp.sum(weights, axis=-1)
    mixed = jnp.einsum(
        "hqk,hkc->hqc", weights.astype(jnp.bfloat16), expanded[..., NOPE:], preferred_element_type=jnp.float32
    )
    head_out = (
        (mixed / denominator[..., None])
        .astype(jnp.bfloat16)
        .transpose(1, 0, 2)
        .reshape(tok_rows, local_heads * VDIM)
    )
    tp_count = lax.axis_size("tp")
    hidden_part = expert_gate_up.shape[3]
    packed = jnp.concatenate(
        [expert_gate_up[0].reshape(2 * D, hidden_part), expert_down[0].T], axis=0
    )
    forward = around(packed, "tp", 1)
    backward = around(packed, "tp", tp_count - 1)
    head_out, forward, backward = lax.optimization_barrier((head_out, forward, backward))
    attn_part = jnp.dot(head_out, o_weight, preferred_element_type=jnp.float32).astype(jnp.bfloat16)
    tp_rank = lax.axis_index("tp")
    share = D // tp_count
    summed = lax.dynamic_slice_in_dim(attn_part, tp_rank * share, share, 1).astype(jnp.float32)
    for d in range(1, tp_count):
        outgoing = lax.dynamic_slice_in_dim(attn_part, ((tp_rank + d) % tp_count) * share, share, 1)
        summed = summed + around(outgoing, "tp", d).astype(jnp.float32)
    hidden_cols = lax.dynamic_slice_in_dim(inputs, tp_rank * share, share, 1) + summed
    hidden_sent = hidden_cols.astype(jnp.bfloat16)
    hidden_rolled = jnp.concatenate(
        [around(hidden_sent, "tp", d).astype(jnp.float32) for d in range(tp_count - 1, 0, -1)]
        + [hidden_cols],
        axis=1,
    )
    hidden = jnp.roll(hidden_rolled, ((tp_rank + 1) % tp_count) * share, axis=1)
    mixed_in = rms_norm(hidden, ffn_gain).astype(jnp.bfloat16)
    shared_act = (
        jax.nn.silu(jnp.dot(mixed_in, shared_gate_up[0], preferred_element_type=jnp.float32))
        * jnp.dot(mixed_in, shared_gate_up[1], preferred_element_type=jnp.float32)
    ).astype(jnp.bfloat16)
    shared_part = jnp.dot(shared_act, shared_down, preferred_element_type=jnp.float32)
    experts = lax.axis_size("seq") * expert_gate_up.shape[0]
    capacity = min(tok_rows, tok_rows * TOPK * 4 // (3 * experts))
    choice_ids = expert_ids.reshape(-1)
    choice_count = choice_ids.shape[0]
    order = jnp.arange(choice_count, dtype=jnp.int32)
    earlier_same = (choice_ids[None, :] == choice_ids[:, None]) & (order[None, :] < order[:, None])
    slot_index = jnp.sum(earlier_same.astype(jnp.int32), axis=1)
    destination = choice_ids * capacity + slot_index
    source_row = order // TOPK
    out_width = mixed_in.shape[1]
    slot_source = jnp.zeros((experts * capacity,), jnp.int32).at[destination].set(source_row)
    tp_share = capacity // tp_count
    my_slots = lax.dynamic_slice_in_dim(
        slot_source.reshape(experts, capacity), tp_rank * tp_share, tp_share, 1
    )
    buffer = mixed_in[my_slots.reshape(-1)].reshape(experts, tp_share, out_width)
    half = packed.shape[0] // 2
    far = jnp.concatenate(
        [around(forward[:half], "tp", 1), around(backward[half:], "tp", tp_count - 1)], axis=0
    )
    weight_parts = [packed, forward, backward, far]
    arrived = lax.all_to_all(buffer, "seq", split_axis=0, concat_axis=0, tiled=True)
    sources = arrived.shape[0]
    flat_rows = arrived.reshape(sources * tp_share, D)
    produced = None
    for part in weight_parts:
        gate_weight = part[:D]
        up_weight = part[D : 2 * D]
        down_weight_t = part[2 * D :]
        activated = (
            jax.nn.silu(jnp.dot(flat_rows, gate_weight, preferred_element_type=jnp.float32))
            * jnp.dot(flat_rows, up_weight, preferred_element_type=jnp.float32)
        ).astype(jnp.bfloat16)
        piece = lax.dot_general(
            activated, down_weight_t, (((1,), (1,)), ((), ())), preferred_element_type=jnp.float32
        ).astype(jnp.bfloat16).astype(jnp.float32)
        produced = piece if produced is None else produced + piece
    produced = produced.astype(jnp.bfloat16).reshape(sources, tp_share, D)
    returned = lax.all_to_all(produced, "seq", split_axis=0, concat_axis=0, tiled=True)
    returned = returned.reshape(experts * tp_share, D).astype(jnp.float32)
    choice_slot = slot_index.reshape(tok_rows, TOPK)
    local_row = choice_ids.reshape(tok_rows, TOPK) * tp_share + choice_slot % tp_share
    mine = (choice_slot // tp_share) == tp_rank
    chosen = local_row[:, :, None] == jnp.arange(experts * tp_share, dtype=jnp.int32)[None, None, :]
    combine = jnp.sum(jnp.where(chosen & mine[:, :, None], route_weight[:, :, None], 0.0), axis=1)
    routed_part = jnp.dot(
        combine, returned, precision=lax.Precision.HIGHEST, preferred_element_type=jnp.float32
    )
    routed = lax.dynamic_slice_in_dim(routed_part, tp_rank * share, share, 1)
    for d in range(1, tp_count):
        outgoing = lax.dynamic_slice_in_dim(routed_part, ((tp_rank + d) % tp_count) * share, share, 1)
        routed = routed + around(outgoing, "tp", d)
    shared_cols = lax.psum_scatter(
        shared_part.astype(jnp.bfloat16), "tp", scatter_dimension=1, tiled=True
    ).astype(jnp.float32)
    return (hidden_cols + shared_cols + routed).astype(jnp.bfloat16)


def solution(mesh):
    placed = (
        P("seq", None),
        P(),
        P(None, "tp"),
        P(),
        P(),
        P(None, "tp"),
        P("tp", None),
        P(),
        P(None, None, "tp"),
        P("tp", None),
        P("seq", None, None, "tp"),
        P("seq", "tp", None),
        P("seq", None),
        P("seq", None),
        P("seq"),
    )
    return jax.shard_map(
        local, mesh=mesh, in_specs=placed, out_specs=P("seq", "tp"), check_vma=False
    )
```
